256 devices in a mesh: region: 8 (over z_lo, core), tile: 32 (over x, z_hi, y).
Axes of the slice: x: 4, y: 4, z: 8 (z_hi: 2, z_lo: 4; z = z_hi * 4 + z_lo), core: 2. Of those that a mesh axis runs over, the one named last changes fastest.
Arguments:
- ens_obs: bfloat16 [32768, 512], P(('region', 'tile')), may hold values from -6 to 6
- obs_values: float32 [32768], P(('region', 'tile')), may hold values from -8 to 8
- obs_var: float32 [32768], P(('region', 'tile')), may hold values from 0.25 to 4
- edge_up: int32 [8192], P(('region', 'tile')), may hold values from 0 to 127
- edge_down: int32 [8192], P(('region', 'tile')), may hold values from 0 to 127
- loc_local: float32 [512, 4096], P(('region', 'tile')), may hold values from 0.02 to 1
- loc_edge: float32 [512, 2048], P(('region', 'tile')), may hold values from 0.02 to 1
- states: bfloat16 [2, 65536, 512], P(None, ('region', 'tile')), may hold values from -6 to 6
- box_ids: int32 [65536], P(('region', 'tile')), may hold values from 0 to 1
Outputs:
- analysis: bfloat16 [2, 65536, 512], P(None, ('region', 'tile'))
The draws below stay inside these ranges and needn't reach their ends.
All inputs are finite; a program needn't handle non-finite values.
Results may differ from the reference program's by a relative error of at most 0.0095.
Values may be sent and summed in bfloat16 or wider, within the bound.
No kernel may reach another device: no remote copies, remote signals or barrier semaphores. Data moves between devices by JAX's collectives and lax.ppermute only.
A program may use at most 128 MiB of HBM per device.

```python
import math
import jax
import jax.numpy as jnp
from jax import lax

K = 512
OBS_DEV = 128
EDGE = 32
BOX_DEV = 2
CELLS_DEV = 256
FIELDS = 2
NOBS = 32768
NCELL = 65536
NBOX = 512
LOCAL_POOL = 4096
EDGE_POOL = 2048
N_REGION = 8
N_TILE = 32


def with_ends(entries, rng, smallest, top_value):
    dims = entries.shape
    place = [jax.random.randint(jax.random.fold_in(rng, axis), (), 0, dims[axis]) for axis in range(len(dims))]
    entries = entries.at[tuple(place)].set(smallest)
    longest = dims.index(max(dims))
    place[longest] = (place[longest] + 1) % dims[longest]
    return entries.at[tuple(place)].set(top_value)


def steps_of(stream_key, shape, pieces, low, largest):
    factor_of, own = 1.0, jax.random.fold_in(stream_key, 6)
    for axis_at, shards_of in pieces:
        heights = jnp.exp(jax.random.uniform(jax.random.fold_in(own, axis_at), (shards_of,), jnp.float32, low / len(pieces), largest / len(pieces)))
        factor_of = factor_of * jnp.repeat(heights, shape[axis_at] // shards_of).reshape([-1 if axis == axis_at else 1 for axis in range(len(shape))])
    return factor_of


def gaussian(stream_key, shape, deviation, limit, cuts=(), kind=jnp.bfloat16):
    drawn = jax.random.normal(stream_key, shape, jnp.float32) * deviation
    if len(cuts) > 0:
        drawn = steps_of(stream_key, shape, cuts, -0.22, 0.18) * drawn
    return jnp.clip(drawn, min=-limit, max=limit).astype(kind)


def setup_inputs(seed: int = 0) -> dict:
    arg_keys = jax.random.split(jax.random.key(seed), 10)
    ens_obs = gaussian(arg_keys[0], (NOBS, K), 1.0, 6.0, ((0, 256),))
    obs_values = gaussian(arg_keys[1], (NOBS,), 1.5, 8.0, ((0, 256),), jnp.float32)
    obs_var = jnp.clip(jnp.exp(math.log(4.0) - 2.7725887 * jax.random.uniform(arg_keys[2], (NOBS,), jnp.float32) ** steps_of(arg_keys[2], (NOBS,), ((0, 256),), -0.2, 0.2)), 0.25, 4.0)
    edge_up = with_ends(jax.random.randint(arg_keys[3], (N_REGION * N_TILE * EDGE,), 0, OBS_DEV), jax.random.fold_in(arg_keys[3], 1), 0, OBS_DEV - 1).astype(jnp.int32)
    edge_down = with_ends(jax.random.randint(arg_keys[4], (N_REGION * N_TILE * EDGE,), 0, OBS_DEV), jax.random.fold_in(arg_keys[4], 1), 0, OBS_DEV - 1).astype(jnp.int32)
    loc_local = jnp.clip(jnp.exp(math.log(1.0) - 3.912023 * jax.random.uniform(arg_keys[5], (NBOX, LOCAL_POOL), jnp.float32) ** steps_of(arg_keys[5], (NBOX, LOCAL_POOL), ((0, 256),), -0.2, 0.2)), 0.02, 1.0)
    loc_edge = jnp.clip(jnp.exp(math.log(1.0) - 3.912023 * jax.random.uniform(arg_keys[6], (NBOX, EDGE_POOL), jnp.float32) ** steps_of(arg_keys[6], (NBOX, EDGE_POOL), ((0, 256),), -0.2, 0.2)), 0.02, 1.0)
    states = gaussian(arg_keys[7], (FIELDS, NCELL, K), 1.0, 6.0, ((1, 256),))
    box_ids = with_ends(jax.random.randint(arg_keys[8], (NCELL,), 0, BOX_DEV), jax.random.fold_in(arg_keys[8], 1), 0, BOX_DEV - 1).astype(jnp.int32)
    return dict(ens_obs=ens_obs, obs_values=obs_values, obs_var=obs_var, edge_up=edge_up, edge_down=edge_down, loc_local=loc_local, loc_edge=loc_edge, states=states, box_ids=box_ids)


def obs_terms(anomaly, obs_info, weights):
    anom_wide = anomaly.astype(jnp.float32)
    obs_scale = weights * obs_info[:, 0].astype(jnp.float32)[None, :]
    scaled = (anom_wide[None] * obs_scale[:, :, None]).astype(jnp.bfloat16)
    scaled = lax.optimization_barrier(scaled).astype(jnp.float32)
    gram_sum = jnp.einsum('bpi,pj->bij', scaled, anom_wide, precision=lax.Precision.HIGHEST)
    weighted = (obs_scale * obs_info[:, 1].astype(jnp.float32)[None, :]).astype(jnp.bfloat16)
    weighted = lax.optimization_barrier(weighted).astype(jnp.float32)
    innov_sum = jnp.einsum('bp,pj->bj', weighted, anom_wide, precision=lax.Precision.HIGHEST)
    return (gram_sum, innov_sum)

def make_transform(gram_sum, innov_sum):
    members = gram_sum.shape[-1]
    identity = jnp.eye(members, dtype=jnp.float32)
    system = gram_sum + (members - 1.0) * identity
    right_sides = jnp.concatenate([jnp.broadcast_to(identity, system.shape), innov_sum[:, :, None]], axis=2)
    solved = jnp.linalg.solve(system, right_sides)
    inverse = solved[:, :, :members]
    wbar = solved[:, :, members]
    transform = 0.5 * identity + 0.5 * (members - 1.0) * inverse + wbar[:, :, None]
    return transform.astype(jnp.bfloat16)

def update_cells(states_dev, boxes_dev, transform):
    wide = states_dev.astype(jnp.float32)
    smean = jnp.mean(wide, axis=2)
    state_anomaly = (wide - smean[:, :, None]).astype(jnp.bfloat16)
    state_anomaly = lax.optimization_barrier(state_anomaly).astype(jnp.float32)
    updates = jnp.einsum('fck,bkj->bfcj', state_anomaly, transform.astype(jnp.float32), precision=lax.Precision.HIGHEST)
    box_range = jnp.arange(transform.shape[0], dtype=jnp.int32)
    selector = (boxes_dev[None, :] == box_range[:, None]).astype(jnp.float32)
    total = jnp.sum(selector[:, None, :, None] * updates, axis=0)
    return (smean[:, :, None] + total).astype(jnp.bfloat16)

def reference(ens_obs, obs_values, obs_var, edge_up, edge_down, loc_local, loc_edge, states, box_ids):
    regions = N_REGION
    tile_count = N_TILE
    wide = ens_obs.astype(jnp.float32).reshape(regions, tile_count, OBS_DEV, K)
    ymean = jnp.mean(wide, axis=3)
    anomaly = (wide - ymean[..., None]).astype(jnp.bfloat16)
    inv_var = 1.0 / obs_var.reshape(regions, tile_count, OBS_DEV)
    innov = obs_values.reshape(regions, tile_count, OBS_DEV) - ymean
    obs_info = jnp.stack([inv_var, innov], axis=-1).astype(jnp.bfloat16)
    up_index = edge_up.reshape(regions, tile_count, EDGE).astype(jnp.int32)
    down_index = edge_down.reshape(regions, tile_count, EDGE).astype(jnp.int32)
    sent_up_a = jnp.take_along_axis(anomaly, up_index[..., None], axis=2)
    sent_up_i = jnp.take_along_axis(obs_info, up_index[..., None], axis=2)
    sent_down_a = jnp.take_along_axis(anomaly, down_index[..., None], axis=2)
    sent_down_i = jnp.take_along_axis(obs_info, down_index[..., None], axis=2)
    lower_a = jnp.concatenate([jnp.zeros_like(sent_up_a[:1]), sent_up_a[:-1]], axis=0)
    lower_i = jnp.concatenate([jnp.zeros_like(sent_up_i[:1]), sent_up_i[:-1]], axis=0)
    upper_a = jnp.concatenate([sent_down_a[1:], jnp.zeros_like(sent_down_a[:1])], axis=0)
    upper_i = jnp.concatenate([sent_down_i[1:], jnp.zeros_like(sent_down_i[:1])], axis=0)
    edge_a = jnp.concatenate([lower_a, upper_a], axis=2)
    edge_i = jnp.concatenate([lower_i, upper_i], axis=2)
    local_w = loc_local.reshape(regions, tile_count, BOX_DEV, LOCAL_POOL)
    edge_w = loc_edge.reshape(regions, tile_count, BOX_DEV, EDGE_POOL)
    states_dev = jnp.transpose(states.reshape(FIELDS, regions, tile_count, CELLS_DEV, K), (1, 2, 0, 3, 4))
    boxes = box_ids.reshape(regions, tile_count, CELLS_DEV).astype(jnp.int32)

    def one_device(index):
        region_at = index // tile_count
        tile_at = index % tile_count
        pool_a = anomaly[region_at].reshape(LOCAL_POOL, K)
        pool_i = obs_info[region_at].reshape(LOCAL_POOL, 2)
        gram_one, innov_one = obs_terms(pool_a, pool_i, local_w[region_at, tile_at])
        rim_a = edge_a[region_at].reshape(EDGE_POOL, K)
        rim_i = edge_i[region_at].reshape(EDGE_POOL, 2)
        gram_two, innov_two = obs_terms(rim_a, rim_i, edge_w[region_at, tile_at])
        transform = make_transform(gram_one + gram_two, innov_one + innov_two)
        return update_cells(states_dev[region_at, tile_at], boxes[region_at, tile_at], transform)
    result = lax.map(one_device, jnp.arange(regions * tile_count, dtype=jnp.int32))
    result = result.reshape(regions, tile_count, FIELDS, CELLS_DEV, K)
    return jnp.transpose(result, (2, 0, 1, 3, 4)).reshape(FIELDS, NCELL, K)
```

```python
import functools

import jax
import jax.numpy as jnp
from jax import lax
from jax.experimental import pallas as pl
from jax.experimental.pallas import tpu as pltpu
from jax.sharding import Mesh
from jax.sharding import PartitionSpec as P

HI = lax.Precision.HIGHEST
ROWS_PER_STEP = 1664


def passed_along(block, axis, distance):
    devices = range(lax.axis_size(axis))
    route = [(i - distance, i) for i in devices if i - distance in devices]
    return lax.ppermute(block, axis, route)


def _gram_kernel(a_ref, s_ref, w_ref, g_ref, v_ref):
    @pl.when(pl.program_id(0) == 0)
    def _():
        g_ref[...] = jnp.zeros(g_ref.shape, jnp.float32)
        v_ref[...] = jnp.zeros(v_ref.shape, jnp.float32)

    a = a_ref[...]
    af = a.astype(jnp.float32)
    for b in range(g_ref.shape[0]):
        sc = (af * s_ref[b]).astype(jnp.bfloat16)
        g_ref[b] += lax.dot_general(sc, a, (((0,), (0,)), ((), ())),
                                    preferred_element_type=jnp.float32)
    v_ref[...] += jnp.dot(w_ref[...], a, preferred_element_type=jnp.float32)


def gram_terms(pool, scale_col, weighted):
    rows, members = pool.shape
    boxes = scale_col.shape[0]
    wrows = weighted.shape[0]
    step = ROWS_PER_STEP
    return pl.pallas_call(
        _gram_kernel,
        grid=(rows // step,),
        in_specs=[
            pl.BlockSpec((step, members), lambda i: (i, 0)),
            pl.BlockSpec((boxes, step, 1), lambda i: (0, i, 0)),
            pl.BlockSpec((wrows, step), lambda i: (0, i)),
        ],
        out_specs=[
            pl.BlockSpec((boxes, members, members), lambda i: (0, 0, 0)),
            pl.BlockSpec((wrows, members), lambda i: (0, 0)),
        ],
        out_shape=[
            jax.ShapeDtypeStruct((boxes, members, members), jnp.float32),
            jax.ShapeDtypeStruct((wrows, members), jnp.float32),
        ],
    )(pool, scale_col, weighted)


def _transform_kernel(g_ref, v_ref, t_ref, m_ref, r_ref, *, nb):
    boxes, n, _ = g_ref.shape
    ridx = lax.broadcasted_iota(jnp.int32, (n, n), 0)
    cidx = lax.broadcasted_iota(jnp.int32, (n, n), 1)
    eye = (ridx == cidx).astype(jnp.float32)
    for b in range(boxes):
        m_ref[b] = g_ref[b] + (n - 1.0) * eye
    bi = lax.broadcasted_iota(jnp.int32, (nb, nb), 0)
    bj = lax.broadcasted_iota(jnp.int32, (nb, nb), 1)
    beye = (bi == bj).astype(jnp.float32)

    def pivot(k, blocks):
        rmask = bi == k
        cmask = bj == k
        out = []
        for d in blocks:
            row = jnp.sum(jnp.where(rmask, d, 0.0), axis=0, keepdims=True)
            col = jnp.sum(jnp.where(cmask, d, 0.0), axis=1, keepdims=True)
            p = jnp.sum(jnp.where(cmask[0:1], row, 0.0), axis=1, keepdims=True)
            pinv = 1.0 / p
            rown = row * pinv
            new = d - col * rown
            new = jnp.where(rmask, rown, new)
            new = jnp.where(cmask, -col * pinv, new)
            new = jnp.where(rmask & cmask, pinv, new)
            out.append(new)
        return tuple(out)

    for kb in range(n // nb):
        s = slice(kb * nb, (kb + 1) * nb)
        dinvs = lax.fori_loop(0, nb, pivot, tuple(m_ref[b, s, s] for b in range(boxes)))
        for b in range(boxes):
            dinv = dinvs[b]
            rn = jnp.dot(dinv, m_ref[b, s, :], precision=HI, preferred_element_type=jnp.float32)
            r_ref[b] = rn
            r_ref[b, :, s] = beye + dinv
            upd = jnp.dot(m_ref[b, :, s], r_ref[b], precision=HI, preferred_element_type=jnp.float32)
            m_ref[b] = m_ref[b] - upd
            m_ref[b, s, :] = rn
            m_ref[b, s, s] = dinv
    for b in range(boxes):
        inv = m_ref[b]
        wbar = jnp.sum(inv * v_ref[b:b + 1, :], axis=1, keepdims=True)
        t_ref[b] = (0.5 * eye + (0.5 * (n - 1.0)) * inv + wbar).astype(t_ref.dtype)


def make_transform(gram, innov_rows, nb=128):
    boxes, n, _ = gram.shape
    return pl.pallas_call(
        functools.partial(_transform_kernel, nb=nb),
        out_shape=jax.ShapeDtypeStruct((boxes, n, n), jnp.bfloat16),
        scratch_shapes=[pltpu.VMEM((boxes, n, n), jnp.float32),
                        pltpu.VMEM((boxes, nb, n), jnp.float32)],
    )(gram, innov_rows)


def body(ens_obs, obs_values, obs_var, edge_up, edge_down, loc_local, loc_edge, states, box_ids):
    record_count, members = ens_obs.shape
    nx, nz, ny = lax.axis_size("tx"), lax.axis_size("tz"), lax.axis_size("ty")
    boxes = loc_local.shape[0]
    ymean = jnp.mean(ens_obs, axis=1, dtype=jnp.float32)
    anomaly = (ens_obs.astype(jnp.float32) - ymean[:, None]).astype(jnp.bfloat16)
    inv_var = (1.0 / obs_var).astype(jnp.bfloat16)
    innov = (obs_values - ymean).astype(jnp.bfloat16)
    lower_a, lower_v, lower_i = passed_along(
        (anomaly[edge_up], inv_var[edge_up], innov[edge_up]), "region", 1)
    upper_a, upper_v, upper_i = passed_along(
        (anomaly[edge_down], inv_var[edge_down], innov[edge_down]), "region", -1)
    edge_rows = lower_a.shape[0] + upper_a.shape[0]
    pool_rows = record_count + edge_rows
    block_rows = ((pool_rows + 1 + 15) // 16) * 16
    info_row = jnp.concatenate(
        [inv_var, lower_v, upper_v, innov, lower_i, upper_i,
         jnp.zeros((members - 2 * pool_rows,), jnp.bfloat16)])
    block = jnp.concatenate(
        [anomaly, lower_a, upper_a, info_row[None],
         jnp.zeros((block_rows - pool_rows - 1, members), jnp.bfloat16)], axis=0)
    half = lax.all_gather(block, "tz", axis=0)
    full = lax.all_gather(half, ("tx", "ty"), axis=0)
    info = full[:, :, pool_rows, :2 * pool_rows].astype(jnp.float32)
    inv_all = info[:, :, :pool_rows]
    innov_all = info[:, :, pool_rows:]
    local_w = loc_local.reshape(boxes, nx, nz, ny, record_count)
    edge_w = loc_edge.reshape(boxes, nx, nz, ny, edge_rows)
    weights = jnp.concatenate([local_w, edge_w], axis=4).transpose(0, 1, 3, 2, 4)
    weights = weights.reshape(boxes, nx * ny, nz, pool_rows)
    obs_scale = weights * inv_all[None]
    weighted = (obs_scale * innov_all[None]).astype(jnp.bfloat16)
    pad = ((0, 0), (0, 0), (0, 0), (0, block_rows - pool_rows))
    scale_col = jnp.pad(obs_scale, pad).reshape(boxes, -1, 1)
    weighted = jnp.pad(weighted, pad).reshape(boxes, -1)
    weighted = jnp.pad(weighted, ((0, 16 - boxes), (0, 0)))
    gram, innov_sum = gram_terms(full.reshape(-1, members), scale_col, weighted)
    transform = make_transform(gram, innov_sum)
    smean = jnp.mean(states, axis=2, dtype=jnp.float32)
    state_anomaly = (states.astype(jnp.float32) - smean[:, :, None]).astype(jnp.bfloat16)
    updates = jnp.einsum(
        "fck,bkj->bfcj", state_anomaly, transform, preferred_element_type=jnp.float32
    )
    box_range = jnp.arange(boxes, dtype=jnp.int32)
    selector = (box_ids[None, :] == box_range[:, None]).astype(jnp.float32)
    total = jnp.sum(selector[:, None, :, None] * updates, axis=0)
    return (smean[:, :, None] + total).astype(jnp.bfloat16)


def solution(mesh):
    n_region, n_tile = mesh.devices.shape
    nz = 2
    nx = 4
    ny = n_tile // (nx * nz)
    fine = Mesh(mesh.devices.reshape(n_region, nx, nz, ny), ("region", "tx", "tz", "ty"))
    flat = ("region", "tx", "tz", "ty")
    return jax.shard_map(
        body,
        mesh=fine,
        in_specs=(
            P(flat, None),
            P(flat),
            P(flat),
            P(flat),
            P(flat),
            P(flat, None),
            P(flat, None),
            P(None, flat, None),
            P(flat),
        ),
        out_specs=P(None, flat, None),
        check_vma=False,
    )
```

```python
import functools

import jax
import jax.numpy as jnp
from jax import lax
from jax.experimental import pallas as pl
from jax.experimental.pallas import tpu as pltpu
from jax.sharding import Mesh
from jax.sharding import PartitionSpec as P

HI = lax.Precision.HIGHEST
ROWS_PER_STEP = 1664


def passed_along(block, axis, distance):
    devices = range(lax.axis_size(axis))
    route = [(i - distance, i) for i in devices if i - distance in devices]
    return lax.ppermute(block, axis, route)


def _gram_kernel(a_ref, s_ref, w_ref, g_ref, v_ref):
    @pl.when(pl.program_id(0) == 0)
    def _():
        g_ref[...] = jnp.zeros(g_ref.shape, jnp.float32)
        v_ref[...] = jnp.zeros(v_ref.shape, jnp.float32)

    a = a_ref[...]
    af = a.astype(jnp.float32)
    sv = s_ref[...]
    lanes = 128
    eye = (lax.broadcasted_iota(jnp.int32, (lanes, lanes), 0)
           == lax.broadcasted_iota(jnp.int32, (lanes, lanes), 1))
    for b in range(g_ref.shape[0]):
        cols = [jnp.sum(jnp.where(eye, sv[b:b + 1, c * lanes:(c + 1) * lanes], 0.0),
                        axis=1, keepdims=True)
                for c in range(a.shape[0] // lanes)]
        sc = (af * jnp.concatenate(cols, axis=0)).astype(jnp.bfloat16)
        g_ref[b] += lax.dot_general(sc, a, (((0,), (0,)), ((), ())),
                                    preferred_element_type=jnp.float32)
    v_ref[...] += jnp.dot(w_ref[...], a, preferred_element_type=jnp.float32)


def gram_terms(pool, scale_rows, weighted, gram_boxes):
    rows, members = pool.shape
    boxes = gram_boxes
    srows = scale_rows.shape[0]
    wrows = weighted.shape[0]
    step = ROWS_PER_STEP
    return pl.pallas_call(
        _gram_kernel,
        grid=(rows // step,),
        in_specs=[
            pl.BlockSpec((step, members), lambda i: (i, 0)),
            pl.BlockSpec((srows, step), lambda i: (0, i)),
            pl.BlockSpec((wrows, step), lambda i: (0, i)),
        ],
        out_specs=[
            pl.BlockSpec((boxes, members, members), lambda i: (0, 0, 0)),
            pl.BlockSpec((wrows, members), lambda i: (0, 0)),
        ],
        out_shape=[
            jax.ShapeDtypeStruct((boxes, members, members), jnp.float32),
            jax.ShapeDtypeStruct((wrows, members), jnp.float32),
        ],
    )(pool, scale_rows, weighted)


def _transform_kernel(g_ref, v_ref, t_ref, m_ref, r_ref, *, nb):
    boxes, n, _ = g_ref.shape
    ridx = lax.broadcasted_iota(jnp.int32, (n, n), 0)
    cidx = lax.broadcasted_iota(jnp.int32, (n, n), 1)
    eye = (ridx == cidx).astype(jnp.float32)
    for b in range(boxes):
        m_ref[b] = g_ref[b] + (n - 1.0) * eye
    bi = lax.broadcasted_iota(jnp.int32, (nb, nb), 0)
    bj = lax.broadcasted_iota(jnp.int32, (nb, nb), 1)
    beye = (bi == bj).astype(jnp.float32)

    def pivot(step, blocks):
        k = 2 * step
        rk, rk1 = bi == k, bi == k + 1
        lk, lk1 = bj[0:1] == k, bj[0:1] == k + 1
        out = []
        for d in blocks:
            r1 = jnp.sum(jnp.where(rk, d, 0.0), axis=0, keepdims=True)
            r2 = jnp.sum(jnp.where(rk1, d, 0.0), axis=0, keepdims=True)
            c1 = jnp.sum(jnp.where(bj == k, d, 0.0), axis=1, keepdims=True)
            c2 = jnp.sum(jnp.where(bj == k + 1, d, 0.0), axis=1, keepdims=True)
            a = jnp.sum(jnp.where(lk, r1, 0.0), axis=1, keepdims=True)
            b = jnp.sum(jnp.where(lk1, r1, 0.0), axis=1, keepdims=True)
            c = jnp.sum(jnp.where(lk, r2, 0.0), axis=1, keepdims=True)
            e = jnp.sum(jnp.where(lk1, r2, 0.0), axis=1, keepdims=True)
            rdet = 1.0 / (a * e - b * c)
            q11, q12, q21, q22 = e * rdet, -b * rdet, -c * rdet, a * rdet
            rn1 = q11 * r1 + q12 * r2
            rn2 = q21 * r1 + q22 * r2
            f1 = jnp.where(lk, 1.0 + q11, jnp.where(lk1, q12, rn1))
            f2 = jnp.where(lk, q21, jnp.where(lk1, 1.0 + q22, rn2))
            g1 = jnp.where(lk, q11, jnp.where(lk1, q12, rn1))
            g2 = jnp.where(lk, q21, jnp.where(lk1, q22, rn2))
            new = d - c1 * f1 - c2 * f2
            out.append(jnp.where(rk, g1, jnp.where(rk1, g2, new)))
        return tuple(out)

    for kb in range(n // nb):
        s = slice(kb * nb, (kb + 1) * nb)
        dinvs = lax.fori_loop(0, nb // 2, pivot, tuple(m_ref[b, s, s] for b in range(boxes)))
        for b in range(boxes):
            dinv = dinvs[b]
            rn = jnp.dot(dinv, m_ref[b, s, :], precision=HI, preferred_element_type=jnp.float32)
            r_ref[b] = rn
            r_ref[b, :, s] = beye + dinv
            upd = jnp.dot(m_ref[b, :, s], r_ref[b], precision=HI, preferred_element_type=jnp.float32)
            m_ref[b] = m_ref[b] - upd
            m_ref[b, s, :] = rn
            m_ref[b, s, s] = dinv
    for b in range(boxes):
        inv = m_ref[b]
        wbar = jnp.sum(inv * v_ref[b:b + 1, :], axis=1, keepdims=True)
        t_ref[b] = (0.5 * eye + (0.5 * (n - 1.0)) * inv + wbar).astype(t_ref.dtype)


def make_transform(gram, innov_rows, nb=128):
    boxes, n, _ = gram.shape
    return pl.pallas_call(
        functools.partial(_transform_kernel, nb=nb),
        out_shape=jax.ShapeDtypeStruct((boxes, n, n), jnp.bfloat16),
        scratch_shapes=[pltpu.VMEM((boxes, n, n), jnp.float32),
                        pltpu.VMEM((boxes, nb, n), jnp.float32)],
    )(gram, innov_rows)


def body(ens_obs, obs_values, obs_var, edge_up, edge_down, loc_local, loc_edge, states, box_ids):
    record_count, members = ens_obs.shape
    nx, nz, ny = lax.axis_size("tx"), lax.axis_size("tz"), lax.axis_size("ty")
    boxes = loc_local.shape[0]
    ymean = jnp.mean(ens_obs, axis=1, dtype=jnp.float32)
    anomaly = (ens_obs.astype(jnp.float32) - ymean[:, None]).astype(jnp.bfloat16)
    inv_var = (1.0 / obs_var).astype(jnp.bfloat16)
    innov = (obs_values - ymean).astype(jnp.bfloat16)
    lower_a, lower_v, lower_i = passed_along(
        (anomaly[edge_up], inv_var[edge_up], innov[edge_up]), "region", 1)
    upper_a, upper_v, upper_i = passed_along(
        (anomaly[edge_down], inv_var[edge_down], innov[edge_down]), "region", -1)
    edge_rows = lower_a.shape[0] + upper_a.shape[0]
    pool_rows = record_count + edge_rows
    block_rows = ((pool_rows + 1 + 15) // 16) * 16
    info_row = jnp.concatenate(
        [inv_var, lower_v, upper_v, innov, lower_i, upper_i,
         jnp.zeros((members - 2 * pool_rows,), jnp.bfloat16)])
    block = jnp.concatenate(
        [anomaly, lower_a, upper_a, info_row[None],
         jnp.zeros((block_rows - pool_rows - 1, members), jnp.bfloat16)], axis=0)
    half = lax.all_gather(block, "tz", axis=0)
    full = lax.all_gather(half, ("tx", "ty"), axis=0)
    info = full[:, :, pool_rows, :2 * pool_rows].astype(jnp.float32)
    inv_all = info[:, :, :pool_rows]
    innov_all = info[:, :, pool_rows:]
    local_w = loc_local.reshape(boxes, nx, nz, ny, record_count)
    edge_w = loc_edge.reshape(boxes, nx, nz, ny, edge_rows)
    weights = jnp.concatenate([local_w, edge_w], axis=4).transpose(0, 1, 3, 2, 4)
    weights = weights.reshape(boxes, nx * ny, nz, pool_rows)
    obs_scale = weights * inv_all[None]
    weighted = (obs_scale * innov_all[None]).astype(jnp.bfloat16)
    pad = ((0, 0), (0, 0), (0, 0), (0, block_rows - pool_rows))
    scale_rows = jnp.pad(obs_scale, pad).reshape(boxes, -1)
    scale_rows = jnp.pad(scale_rows, ((0, 8 - boxes), (0, 0)))
    weighted = jnp.pad(weighted, pad).reshape(boxes, -1)
    weighted = jnp.pad(weighted, ((0, 16 - boxes), (0, 0)))
    gram, innov_sum = gram_terms(full.reshape(-1, members), scale_rows, weighted, boxes)
    transform = make_transform(gram, innov_sum)
    smean = jnp.mean(states, axis=2, dtype=jnp.float32)
    state_anomaly = (states.astype(jnp.float32) - smean[:, :, None]).astype(jnp.bfloat16)
    updates = jnp.einsum(
        "fck,bkj->bfcj", state_anomaly, transform, preferred_element_type=jnp.float32
    )
    box_range = jnp.arange(boxes, dtype=jnp.int32)
    selector = (box_ids[None, :] == box_range[:, None]).astype(jnp.float32)
    total = jnp.sum(selector[:, None, :, None] * updates, axis=0)
    return (smean[:, :, None] + total).astype(jnp.bfloat16)


def solution(mesh):
    n_region, n_tile = mesh.devices.shape
    nz = 2
    nx = 4
    ny = n_tile // (nx * nz)
    fine = Mesh(mesh.devices.reshape(n_region, nx, nz, ny), ("region", "tx", "tz", "ty"))
    flat = ("region", "tx", "tz", "ty")
    return jax.shard_map(
        body,
        mesh=fine,
        in_specs=(
            P(flat, None),
            P(flat),
            P(flat),
            P(flat),
            P(flat),
            P(flat, None),
            P(flat, None),
            P(None, flat, None),
            P(flat),
        ),
        out_specs=P(None, flat, None),
        check_vma=False,
    )
```

```python
import functools

import jax
import jax.numpy as jnp
from jax import lax
from jax.experimental import pallas as pl
from jax.experimental.pallas import tpu as pltpu
from jax.sharding import Mesh
from jax.sharding import PartitionSpec as P

HI = lax.Precision.HIGHEST
ROWS_PER_STEP = 1664


def passed_along(block, axis, distance):
    devices = range(lax.axis_size(axis))
    route = [(i - distance, i) for i in devices if i - distance in devices]
    return lax.ppermute(block, axis, route)


def _gram_kernel(a_ref, s_ref, w_ref, g_ref, v_ref):
    @pl.when(pl.program_id(0) == 0)
    def _():
        g_ref[...] = jnp.zeros(g_ref.shape, jnp.float32)
        v_ref[...] = jnp.zeros(v_ref.shape, jnp.float32)

    a = a_ref[...]
    af = a.astype(jnp.float32)
    sv = s_ref[...]
    lanes = 128
    eye = (lax.broadcasted_iota(jnp.int32, (lanes, lanes), 0)
           == lax.broadcasted_iota(jnp.int32, (lanes, lanes), 1))
    for b in range(g_ref.shape[0]):
        cols = [jnp.sum(jnp.where(eye, sv[b:b + 1, c * lanes:(c + 1) * lanes], 0.0),
                        axis=1, keepdims=True)
                for c in range(a.shape[0] // lanes)]
        sc = (af * jnp.concatenate(cols, axis=0)).astype(jnp.bfloat16)
        g_ref[b] += lax.dot_general(sc, a, (((0,), (0,)), ((), ())),
                                    preferred_element_type=jnp.float32)
    v_ref[...] += jnp.dot(w_ref[...], a, preferred_element_type=jnp.float32)


def gram_terms(pool, scale_rows, weighted, gram_boxes):
    rows, members = pool.shape
    boxes = gram_boxes
    srows = scale_rows.shape[0]
    wrows = weighted.shape[0]
    step = ROWS_PER_STEP
    return pl.pallas_call(
        _gram_kernel,
        grid=(rows // step,),
        in_specs=[
            pl.BlockSpec((step, members), lambda i: (i, 0)),
            pl.BlockSpec((srows, step), lambda i: (0, i)),
            pl.BlockSpec((wrows, step), lambda i: (0, i)),
        ],
        out_specs=[
            pl.BlockSpec((boxes, members, members), lambda i: (0, 0, 0)),
            pl.BlockSpec((wrows, members), lambda i: (0, 0)),
        ],
        out_shape=[
            jax.ShapeDtypeStruct((boxes, members, members), jnp.float32),
            jax.ShapeDtypeStruct((wrows, members), jnp.float32),
        ],
    )(pool, scale_rows, weighted)


def _transform_kernel(g_ref, v_ref, t_ref, m_ref, r_ref, *, nb):
    boxes, n, _ = g_ref.shape
    ridx = lax.broadcasted_iota(jnp.int32, (n, n), 0)
    cidx = lax.broadcasted_iota(jnp.int32, (n, n), 1)
    eye = (ridx == cidx).astype(jnp.float32)
    for b in range(boxes):
        m_ref[b] = g_ref[b] + (n - 1.0) * eye
    bi = lax.broadcasted_iota(jnp.int32, (nb, nb), 0)
    bj = lax.broadcasted_iota(jnp.int32, (nb, nb), 1)
    beye = (bi == bj).astype(jnp.float32)

    def pivot(step, blocks):
        k = 2 * step
        rk, rk1 = bi == k, bi == k + 1
        lk, lk1 = bj[0:1] == k, bj[0:1] == k + 1
        out = []
        for d in blocks:
            r1 = jnp.sum(jnp.where(rk, d, 0.0), axis=0, keepdims=True)
            r2 = jnp.sum(jnp.where(rk1, d, 0.0), axis=0, keepdims=True)
            c1 = jnp.sum(jnp.where(bj == k, d, 0.0), axis=1, keepdims=True)
            c2 = jnp.sum(jnp.where(bj == k + 1, d, 0.0), axis=1, keepdims=True)
            a = jnp.sum(jnp.where(lk, r1, 0.0), axis=1, keepdims=True)
            b = jnp.sum(jnp.where(lk1, r1, 0.0), axis=1, keepdims=True)
            c = jnp.sum(jnp.where(lk, r2, 0.0), axis=1, keepdims=True)
            e = jnp.sum(jnp.where(lk1, r2, 0.0), axis=1, keepdims=True)
            rdet = 1.0 / (a * e - b * c)
            q11, q12, q21, q22 = e * rdet, -b * rdet, -c * rdet, a * rdet
            rn1 = q11 * r1 + q12 * r2
            rn2 = q21 * r1 + q22 * r2
            f1 = jnp.where(lk, 1.0 + q11, jnp.where(lk1, q12, rn1))
            f2 = jnp.where(lk, q21, jnp.where(lk1, 1.0 + q22, rn2))
            g1 = jnp.where(lk, q11, jnp.where(lk1, q12, rn1))
            g2 = jnp.where(lk, q21, jnp.where(lk1, q22, rn2))
            new = d - c1 * f1 - c2 * f2
            out.append(jnp.where(rk, g1, jnp.where(rk1, g2, new)))
        return tuple(out)

    for kb in range(n // nb):
        s = slice(kb * nb, (kb + 1) * nb)
        dinvs = lax.fori_loop(0, nb // 2, pivot, tuple(m_ref[b, s, s] for b in range(boxes)))
        for b in range(boxes):
            dinv = dinvs[b]
            rn = jnp.dot(dinv, m_ref[b, s, :], precision=HI, preferred_element_type=jnp.float32)
            r_ref[b] = rn
            r_ref[b, :, s] = beye + dinv
            upd = jnp.dot(m_ref[b, :, s], r_ref[b], precision=HI, preferred_element_type=jnp.float32)
            m_ref[b] = m_ref[b] - upd
            m_ref[b, s, :] = rn
            m_ref[b, s, s] = dinv
    for b in range(boxes):
        inv = m_ref[b]
        wbar = jnp.sum(inv * v_ref[b:b + 1, :], axis=1, keepdims=True)
        t_ref[b] = (0.5 * eye + (0.5 * (n - 1.0)) * inv + wbar).astype(t_ref.dtype)


def make_transform(gram, innov_rows, nb=128):
    boxes, n, _ = gram.shape
    return pl.pallas_call(
        functools.partial(_transform_kernel, nb=nb),
        out_shape=jax.ShapeDtypeStruct((boxes, n, n), jnp.bfloat16),
        scratch_shapes=[pltpu.VMEM((boxes, n, n), jnp.float32),
                        pltpu.VMEM((boxes, nb, n), jnp.float32)],
    )(gram, innov_rows)


def body(ens_obs, obs_values, obs_var, edge_up, edge_down, loc_local, loc_edge, states, box_ids):
    record_count, members = ens_obs.shape
    nx, nz, ny = lax.axis_size("tx"), lax.axis_size("tz"), lax.axis_size("ty")
    boxes = loc_local.shape[0]
    ymean = jnp.mean(ens_obs, axis=1, dtype=jnp.float32)
    anomaly = (ens_obs.astype(jnp.float32) - ymean[:, None]).astype(jnp.bfloat16)
    inv_var = (1.0 / obs_var).astype(jnp.bfloat16)
    innov = (obs_values - ymean).astype(jnp.bfloat16)
    lower_a, lower_v, lower_i = passed_along(
        (anomaly[edge_up], inv_var[edge_up], innov[edge_up]), "region", 1)
    upper_a, upper_v, upper_i = passed_along(
        (anomaly[edge_down], inv_var[edge_down], innov[edge_down]), "region", -1)
    edge_rows = lower_a.shape[0] + upper_a.shape[0]
    pool_rows = record_count + edge_rows
    block_rows = ((pool_rows + 1 + 15) // 16) * 16
    info_row = jnp.concatenate(
        [inv_var, lower_v, upper_v, innov, lower_i, upper_i,
         jnp.zeros((members - 2 * pool_rows,), jnp.bfloat16)])
    block = jnp.concatenate(
        [anomaly, lower_a, upper_a, info_row[None],
         jnp.zeros((block_rows - pool_rows - 1, members), jnp.bfloat16)], axis=0)
    half = lax.all_gather(block, "tz", axis=0)
    first = lax.all_gather(lax.all_gather(half[0], "tx", axis=0), "ty", axis=0)
    second = lax.all_gather(lax.all_gather(half[1], "ty", axis=0), "tx", axis=0)
    local_w = loc_local.reshape(boxes, nx, nz, ny, record_count)
    edge_w = loc_edge.reshape(boxes, nx, nz, ny, edge_rows)
    weights = jnp.concatenate([local_w, edge_w], axis=4)
    parts = ((first, weights[:, :, 0].transpose(0, 2, 1, 3)), (second, weights[:, :, 1]))
    gram = innov_sum = None
    for pool, w in parts:
        info = pool[:, :, pool_rows, :2 * pool_rows].astype(jnp.float32)
        obs_scale = w * info[None, :, :, :pool_rows]
        weighted = (obs_scale * info[None, :, :, pool_rows:]).astype(jnp.bfloat16)
        pad = ((0, 0), (0, 0), (0, 0), (0, block_rows - pool_rows))
        scale_rows = jnp.pad(obs_scale, pad).reshape(boxes, -1)
        scale_rows = jnp.pad(scale_rows, ((0, 8 - boxes), (0, 0)))
        weighted = jnp.pad(weighted, pad).reshape(boxes, -1)
        weighted = jnp.pad(weighted, ((0, 16 - boxes), (0, 0)))
        g, v = gram_terms(pool.reshape(-1, members), scale_rows, weighted, boxes)
        gram = g if gram is None else gram + g
        innov_sum = v if innov_sum is None else innov_sum + v
    transform = make_transform(gram, innov_sum)
    smean = jnp.mean(states, axis=2, dtype=jnp.float32)
    state_anomaly = (states.astype(jnp.float32) - smean[:, :, None]).astype(jnp.bfloat16)
    updates = jnp.einsum(
        "fck,bkj->bfcj", state_anomaly, transform, preferred_element_type=jnp.float32
    )
    box_range = jnp.arange(boxes, dtype=jnp.int32)
    selector = (box_ids[None, :] == box_range[:, None]).astype(jnp.float32)
    total = jnp.sum(selector[:, None, :, None] * updates, axis=0)
    return (smean[:, :, None] + total).astype(jnp.bfloat16)


def solution(mesh):
    n_region, n_tile = mesh.devices.shape
    nz = 2
    nx = 4
    ny = n_tile // (nx * nz)
    fine = Mesh(mesh.devices.reshape(n_region, nx, nz, ny), ("region", "tx", "tz", "ty"))
    flat = ("region", "tx", "tz", "ty")
    return jax.shard_map(
        body,
        mesh=fine,
        in_specs=(
            P(flat, None),
            P(flat),
            P(flat),
            P(flat),
            P(flat),
            P(flat, None),
            P(flat, None),
            P(None, flat, None),
            P(flat),
        ),
        out_specs=P(None, flat, None),
        check_vma=False,
    )
```

```python
import functools

import jax
import jax.numpy as jnp
from jax import lax
from jax.experimental import pallas as pl
from jax.experimental.pallas import tpu as pltpu
from jax.sharding import Mesh
from jax.sharding import PartitionSpec as P

HI = lax.Precision.HIGHEST
ROWS_PER_STEP = 1664


def passed_along(block, axis, distance):
    devices = range(lax.axis_size(axis))
    route = [(i - distance, i) for i in devices if i - distance in devices]
    return lax.ppermute(block, axis, route)


def _gram_kernel(a_ref, s_ref, w_ref, g_ref, v_ref):
    @pl.when(pl.program_id(0) == 0)
    def _():
        g_ref[...] = jnp.zeros(g_ref.shape, jnp.float32)
        v_ref[...] = jnp.zeros(v_ref.shape, jnp.float32)

    a = a_ref[...]
    af = a.astype(jnp.float32)
    sv = s_ref[...]
    lanes = 128
    eye = (lax.broadcasted_iota(jnp.int32, (lanes, lanes), 0)
           == lax.broadcasted_iota(jnp.int32, (lanes, lanes), 1))
    for b in range(g_ref.shape[0]):
        cols = [jnp.sum(jnp.where(eye, sv[b:b + 1, c * lanes:(c + 1) * lanes], 0.0),
                        axis=1, keepdims=True)
                for c in range(a.shape[0] // lanes)]
        sc = (af * jnp.concatenate(cols, axis=0)).astype(jnp.bfloat16)
        g_ref[b] += lax.dot_general(sc, a, (((0,), (0,)), ((), ())),
                                    preferred_element_type=jnp.float32)
    v_ref[...] += jnp.dot(w_ref[...], a, preferred_element_type=jnp.float32)


def gram_terms(pool, scale_rows, weighted, gram_boxes):
    rows, members = pool.shape
    boxes = gram_boxes
    srows = scale_rows.shape[0]
    wrows = weighted.shape[0]
    step = ROWS_PER_STEP
    return pl.pallas_call(
        _gram_kernel,
        grid=(rows // step,),
        in_specs=[
            pl.BlockSpec((step, members), lambda i: (i, 0)),
            pl.BlockSpec((srows, step), lambda i: (0, i)),
            pl.BlockSpec((wrows, step), lambda i: (0, i)),
        ],
        out_specs=[
            pl.BlockSpec((boxes, members, members), lambda i: (0, 0, 0)),
            pl.BlockSpec((wrows, members), lambda i: (0, 0)),
        ],
        out_shape=[
            jax.ShapeDtypeStruct((boxes, members, members), jnp.float32),
            jax.ShapeDtypeStruct((wrows, members), jnp.float32),
        ],
    )(pool, scale_rows, weighted)


def _transform_kernel(g_ref, v_ref, t_ref, m_ref, r_ref, *, nb):
    boxes, n, _ = g_ref.shape
    ridx = lax.broadcasted_iota(jnp.int32, (n, n), 0)
    cidx = lax.broadcasted_iota(jnp.int32, (n, n), 1)
    eye = (ridx == cidx).astype(jnp.float32)
    for b in range(boxes):
        m_ref[b] = g_ref[b] + (n - 1.0) * eye
    bi = lax.broadcasted_iota(jnp.int32, (nb, nb), 0)
    bj = lax.broadcasted_iota(jnp.int32, (nb, nb), 1)
    beye = (bi == bj).astype(jnp.float32)

    def pivot(step, blocks):
        k = 2 * step
        rk, rk1 = bi == k, bi == k + 1
        lk, lk1 = bj[0:1] == k, bj[0:1] == k + 1
        out = []
        for d in blocks:
            r1 = jnp.sum(jnp.where(rk, d, 0.0), axis=0, keepdims=True)
            r2 = jnp.sum(jnp.where(rk1, d, 0.0), axis=0, keepdims=True)
            c1 = jnp.sum(jnp.where(bj == k, d, 0.0), axis=1, keepdims=True)
            c2 = jnp.sum(jnp.where(bj == k + 1, d, 0.0), axis=1, keepdims=True)
            a = jnp.sum(jnp.where(lk, r1, 0.0), axis=1, keepdims=True)
            b = jnp.sum(jnp.where(lk1, r1, 0.0), axis=1, keepdims=True)
            c = jnp.sum(jnp.where(lk, r2, 0.0), axis=1, keepdims=True)
            e = jnp.sum(jnp.where(lk1, r2, 0.0), axis=1, keepdims=True)
            rdet = 1.0 / (a * e - b * c)
            q11, q12, q21, q22 = e * rdet, -b * rdet, -c * rdet, a * rdet
            rn1 = q11 * r1 + q12 * r2
            rn2 = q21 * r1 + q22 * r2
            f1 = jnp.where(lk, 1.0 + q11, jnp.where(lk1, q12, rn1))
            f2 = jnp.where(lk, q21, jnp.where(lk1, 1.0 + q22, rn2))
            g1 = jnp.where(lk, q11, jnp.where(lk1, q12, rn1))
            g2 = jnp.where(lk, q21, jnp.where(lk1, q22, rn2))
            new = d - c1 * f1 - c2 * f2
            out.append(jnp.where(rk, g1, jnp.where(rk1, g2, new)))
        return tuple(out)

    for kb in range(n // nb):
        s = slice(kb * nb, (kb + 1) * nb)
        dinvs = lax.fori_loop(0, nb // 2, pivot, tuple(m_ref[b, s, s] for b in range(boxes)))
        for b in range(boxes):
            dinv = dinvs[b]
            rn = jnp.dot(dinv, m_ref[b, s, :], precision=HI, preferred_element_type=jnp.float32)
            r_ref[b] = rn
            r_ref[b, :, s] = beye + dinv
            upd = jnp.dot(m_ref[b, :, s], r_ref[b], precision=HI, preferred_element_type=jnp.float32)
            m_ref[b] = m_ref[b] - upd
            m_ref[b, s, :] = rn
            m_ref[b, s, s] = dinv
    for b in range(boxes):
        inv = m_ref[b]
        wbar = jnp.sum(inv * v_ref[b:b + 1, :], axis=1, keepdims=True)
        t_ref[b] = (0.5 * eye + (0.5 * (n - 1.0)) * inv + wbar).astype(t_ref.dtype)


def make_transform(gram, innov_rows, nb=128):
    boxes, n, _ = gram.shape
    return pl.pallas_call(
        functools.partial(_transform_kernel, nb=nb),
        out_shape=jax.ShapeDtypeStruct((boxes, n, n), jnp.bfloat16),
        scratch_shapes=[pltpu.VMEM((boxes, n, n), jnp.float32),
                        pltpu.VMEM((boxes, nb, n), jnp.float32)],
    )(gram, innov_rows)


def body(ens_obs, obs_values, obs_var, edge_up, edge_down, loc_local, loc_edge, states, box_ids):
    record_count, members = ens_obs.shape
    nx, nz, ny = lax.axis_size("tx"), lax.axis_size("tz"), lax.axis_size("ty")
    boxes = loc_local.shape[0]
    ymean = jnp.mean(ens_obs, axis=1, dtype=jnp.float32)
    anomaly = (ens_obs.astype(jnp.float32) - ymean[:, None]).astype(jnp.bfloat16)
    inv_var = (1.0 / obs_var).astype(jnp.bfloat16)
    innov = (obs_values - ymean).astype(jnp.bfloat16)
    def edge_payload(index):
        info = jnp.concatenate([inv_var[index], innov[index]])
        info = jnp.pad(info, (0, members - info.shape[0]))
        return jnp.concatenate([anomaly[index], info[None]], axis=0)

    lower = passed_along(edge_payload(edge_up), "region", 1)
    upper = passed_along(edge_payload(edge_down), "region", -1)
    edge = edge_up.shape[0]
    lower_a, lower_v, lower_i = lower[:edge], lower[edge, :edge], lower[edge, edge:2 * edge]
    upper_a, upper_v, upper_i = upper[:edge], upper[edge, :edge], upper[edge, edge:2 * edge]
    edge_rows = lower_a.shape[0] + upper_a.shape[0]
    pool_rows = record_count + edge_rows
    block_rows = ((pool_rows + 1 + 15) // 16) * 16
    info_row = jnp.concatenate(
        [inv_var, lower_v, upper_v, innov, lower_i, upper_i,
         jnp.zeros((members - 2 * pool_rows,), jnp.bfloat16)])
    block = jnp.concatenate(
        [anomaly, lower_a, upper_a, info_row[None],
         jnp.zeros((block_rows - pool_rows - 1, members), jnp.bfloat16)], axis=0)
    half = lax.all_gather(block, "tz", axis=0)
    full = lax.all_gather(half, ("tx", "ty"), axis=0)
    info = full[:, :, pool_rows, :2 * pool_rows].astype(jnp.float32)
    inv_all = info[:, :, :pool_rows]
    innov_all = info[:, :, pool_rows:]
    local_w = loc_local.reshape(boxes, nx, nz, ny, record_count)
    edge_w = loc_edge.reshape(boxes, nx, nz, ny, edge_rows)
    weights = jnp.concatenate([local_w, edge_w], axis=4).transpose(0, 1, 3, 2, 4)
    weights = weights.reshape(boxes, nx * ny, nz, pool_rows)
    obs_scale = weights * inv_all[None]
    weighted = (obs_scale * innov_all[None]).astype(jnp.bfloat16)
    pad = ((0, 0), (0, 0), (0, 0), (0, block_rows - pool_rows))
    scale_rows = jnp.pad(obs_scale, pad).reshape(boxes, -1)
    scale_rows = jnp.pad(scale_rows, ((0, 8 - boxes), (0, 0)))
    weighted = jnp.pad(weighted, pad).reshape(boxes, -1)
    weighted = jnp.pad(weighted, ((0, 16 - boxes), (0, 0)))
    gram, innov_sum = gram_terms(full.reshape(-1, members), scale_rows, weighted, boxes)
    transform = make_transform(gram, innov_sum)
    smean = jnp.mean(states, axis=2, dtype=jnp.float32)
    state_anomaly = (states.astype(jnp.float32) - smean[:, :, None]).astype(jnp.bfloat16)
    updates = jnp.einsum(
        "fck,bkj->bfcj", state_anomaly, transform, preferred_element_type=jnp.float32
    )
    box_range = jnp.arange(boxes, dtype=jnp.int32)
    selector = (box_ids[None, :] == box_range[:, None]).astype(jnp.float32)
    total = jnp.sum(selector[:, None, :, None] * updates, axis=0)
    return (smean[:, :, None] + total).astype(jnp.bfloat16)


def solution(mesh):
    n_region, n_tile = mesh.devices.shape
    nz = 2
    nx = 4
    ny = n_tile // (nx * nz)
    fine = Mesh(mesh.devices.reshape(n_region, nx, nz, ny), ("region", "tx", "tz", "ty"))
    flat = ("region", "tx", "tz", "ty")
    return jax.shard_map(
        body,
        mesh=fine,
        in_specs=(
            P(flat, None),
            P(flat),
            P(flat),
            P(flat),
            P(flat),
            P(flat, None),
            P(flat, None),
            P(None, flat, None),
            P(flat),
        ),
        out_specs=P(None, flat, None),
        check_vma=False,
    )
```

```python
import functools

import jax
import jax.numpy as jnp
from jax import lax
from jax.experimental import pallas as pl
from jax.experimental.pallas import tpu as pltpu
from jax.sharding import Mesh
from jax.sharding import PartitionSpec as P

HI = lax.Precision.HIGHEST
ROWS_PER_STEP = 1664


def passed_along(block, axis, distance):
    devices = range(lax.axis_size(axis))
    route = [(i - distance, i) for i in devices if i - distance in devices]
    return lax.ppermute(block, axis, route)


def ring_gather(block, axis):
    size = lax.axis_size(axis)
    ahead = [(i, (i + 1) % size) for i in range(size)]
    behind = [(i, (i - 1) % size) for i in range(size)]
    from_prev = lax.ppermute(block, axis, ahead)
    from_next = lax.ppermute(block, axis, behind)
    cut = block.shape[0] // 2
    far = jnp.concatenate([lax.ppermute(from_prev[:cut], axis, ahead),
                           lax.ppermute(from_next[cut:], axis, behind)], axis=0)
    return jnp.stack([block, from_prev, far, from_next], axis=0)


def _gram_kernel(a_ref, s_ref, w_ref, g_ref, v_ref):
    @pl.when(pl.program_id(0) == 0)
    def _():
        g_ref[...] = jnp.zeros(g_ref.shape, jnp.float32)
        v_ref[...] = jnp.zeros(v_ref.shape, jnp.float32)

    a = a_ref[...]
    af = a.astype(jnp.float32)
    sv = s_ref[...]
    lanes = 128
    eye = (lax.broadcasted_iota(jnp.int32, (lanes, lanes), 0)
           == lax.broadcasted_iota(jnp.int32, (lanes, lanes), 1))
    for b in range(g_ref.shape[0]):
        cols = [jnp.sum(jnp.where(eye, sv[b:b + 1, c * lanes:(c + 1) * lanes], 0.0),
                        axis=1, keepdims=True)
                for c in range(a.shape[0] // lanes)]
        sc = (af * jnp.concatenate(cols, axis=0)).astype(jnp.bfloat16)
        g_ref[b] += lax.dot_general(sc, a, (((0,), (0,)), ((), ())),
                                    preferred_element_type=jnp.float32)
    v_ref[...] += jnp.dot(w_ref[...], a, preferred_element_type=jnp.float32)


def gram_terms(pool, scale_rows, weighted, gram_boxes):
    rows, members = pool.shape
    boxes = gram_boxes
    srows = scale_rows.shape[0]
    wrows = weighted.shape[0]
    step = ROWS_PER_STEP
    return pl.pallas_call(
        _gram_kernel,
        grid=(rows // step,),
        in_specs=[
            pl.BlockSpec((step, members), lambda i: (i, 0)),
            pl.BlockSpec((srows, step), lambda i: (0, i)),
            pl.BlockSpec((wrows, step), lambda i: (0, i)),
        ],
        out_specs=[
            pl.BlockSpec((boxes, members, members), lambda i: (0, 0, 0)),
            pl.BlockSpec((wrows, members), lambda i: (0, 0)),
        ],
        out_shape=[
            jax.ShapeDtypeStruct((boxes, members, members), jnp.float32),
            jax.ShapeDtypeStruct((wrows, members), jnp.float32),
        ],
    )(pool, scale_rows, weighted)


def _transform_kernel(g_ref, v_ref, t_ref, m_ref, r_ref, *, nb):
    boxes, n, _ = g_ref.shape
    ridx = lax.broadcasted_iota(jnp.int32, (n, n), 0)
    cidx = lax.broadcasted_iota(jnp.int32, (n, n), 1)
    eye = (ridx == cidx).astype(jnp.float32)
    for b in range(boxes):
        m_ref[b] = g_ref[b] + (n - 1.0) * eye
    bi = lax.broadcasted_iota(jnp.int32, (nb, nb), 0)
    bj = lax.broadcasted_iota(jnp.int32, (nb, nb), 1)
    beye = (bi == bj).astype(jnp.float32)

    def pivot(step, blocks):
        k = 2 * step
        rk, rk1 = bi == k, bi == k + 1
        lk, lk1 = bj[0:1] == k, bj[0:1] == k + 1
        out = []
        for d in blocks:
            r1 = jnp.sum(jnp.where(rk, d, 0.0), axis=0, keepdims=True)
            r2 = jnp.sum(jnp.where(rk1, d, 0.0), axis=0, keepdims=True)
            c1 = jnp.sum(jnp.where(bj == k, d, 0.0), axis=1, keepdims=True)
            c2 = jnp.sum(jnp.where(bj == k + 1, d, 0.0), axis=1, keepdims=True)
            a = jnp.sum(jnp.where(lk, r1, 0.0), axis=1, keepdims=True)
            b = jnp.sum(jnp.where(lk1, r1, 0.0), axis=1, keepdims=True)
            c = jnp.sum(jnp.where(lk, r2, 0.0), axis=1, keepdims=True)
            e = jnp.sum(jnp.where(lk1, r2, 0.0), axis=1, keepdims=True)
            rdet = 1.0 / (a * e - b * c)
            q11, q12, q21, q22 = e * rdet, -b * rdet, -c * rdet, a * rdet
            rn1 = q11 * r1 + q12 * r2
            rn2 = q21 * r1 + q22 * r2
            f1 = jnp.where(lk, 1.0 + q11, jnp.where(lk1, q12, rn1))
            f2 = jnp.where(lk, q21, jnp.where(lk1, 1.0 + q22, rn2))
            g1 = jnp.where(lk, q11, jnp.where(lk1, q12, rn1))
            g2 = jnp.where(lk, q21, jnp.where(lk1, q22, rn2))
            new = d - c1 * f1 - c2 * f2
            out.append(jnp.where(rk, g1, jnp.where(rk1, g2, new)))
        return tuple(out)

    for kb in range(n // nb):
        s = slice(kb * nb, (kb + 1) * nb)
        dinvs = lax.fori_loop(0, nb // 2, pivot, tuple(m_ref[b, s, s] for b in range(boxes)))
        for b in range(boxes):
            dinv = dinvs[b]
            rn = jnp.dot(dinv, m_ref[b, s, :], precision=HI, preferred_element_type=jnp.float32)
            r_ref[b] = rn
            r_ref[b, :, s] = beye + dinv
            upd = jnp.dot(m_ref[b, :, s], r_ref[b], precision=HI, preferred_element_type=jnp.float32)
            m_ref[b] = m_ref[b] - upd
            m_ref[b, s, :] = rn
            m_ref[b, s, s] = dinv
    for b in range(boxes):
        inv = m_ref[b]
        wbar = jnp.sum(inv * v_ref[b:b + 1, :], axis=1, keepdims=True)
        t_ref[b] = (0.5 * eye + (0.5 * (n - 1.0)) * inv + wbar).astype(t_ref.dtype)


def make_transform(gram, innov_rows, nb=128):
    boxes, n, _ = gram.shape
    return pl.pallas_call(
        functools.partial(_transform_kernel, nb=nb),
        out_shape=jax.ShapeDtypeStruct((boxes, n, n), jnp.bfloat16),
        scratch_shapes=[pltpu.VMEM((boxes, n, n), jnp.float32),
                        pltpu.VMEM((boxes, nb, n), jnp.float32)],
    )(gram, innov_rows)


def body(ens_obs, obs_values, obs_var, edge_up, edge_down, loc_local, loc_edge, states, box_ids):
    record_count, members = ens_obs.shape
    nx, nz, ny = lax.axis_size("tx"), lax.axis_size("tz"), lax.axis_size("ty")
    boxes = loc_local.shape[0]
    ymean = jnp.mean(ens_obs, axis=1, dtype=jnp.float32)
    anomaly = (ens_obs.astype(jnp.float32) - ymean[:, None]).astype(jnp.bfloat16)
    inv_var = (1.0 / obs_var).astype(jnp.bfloat16)
    innov = (obs_values - ymean).astype(jnp.bfloat16)
    def edge_payload(index):
        info = jnp.concatenate([inv_var[index], innov[index]])
        info = jnp.pad(info, (0, members - info.shape[0]))
        return jnp.concatenate([anomaly[index], info[None]], axis=0)

    lower = passed_along(edge_payload(edge_up), "region", 1)
    upper = passed_along(edge_payload(edge_down), "region", -1)
    edge = edge_up.shape[0]
    lower_a, lower_v, lower_i = lower[:edge], lower[edge, :edge], lower[edge, edge:2 * edge]
    upper_a, upper_v, upper_i = upper[:edge], upper[edge, :edge], upper[edge, edge:2 * edge]
    edge_rows = lower_a.shape[0] + upper_a.shape[0]
    pool_rows = record_count + edge_rows
    block_rows = ((pool_rows + 1 + 15) // 16) * 16
    info_row = jnp.concatenate(
        [inv_var, lower_v, upper_v, innov, lower_i, upper_i,
         jnp.zeros((members - 2 * pool_rows,), jnp.bfloat16)])
    block = jnp.concatenate(
        [anomaly, lower_a, upper_a, info_row[None],
         jnp.zeros((block_rows - pool_rows - 1, members), jnp.bfloat16)], axis=0)
    half = lax.all_gather(block, "tz", axis=0)
    first = ring_gather(ring_gather(half[0], "tx"), "ty")
    second = ring_gather(ring_gather(half[1], "ty"), "tx")
    full = jnp.stack([first, second.transpose(1, 0, 2, 3)], axis=2)
    full = full.reshape(ny * nx, nz, block_rows, members)
    info = full[:, :, pool_rows, :2 * pool_rows].astype(jnp.float32)
    inv_all = info[:, :, :pool_rows]
    innov_all = info[:, :, pool_rows:]
    local_w = loc_local.reshape(boxes, nx, nz, ny, record_count)
    edge_w = loc_edge.reshape(boxes, nx, nz, ny, edge_rows)
    weights = jnp.concatenate([local_w, edge_w], axis=4)
    x_at, y_at = lax.axis_index("tx"), lax.axis_index("ty")
    x_src = (x_at - jnp.arange(nx)) % nx
    y_src = (y_at - jnp.arange(ny)) % ny
    weights = jnp.take(weights, x_src, axis=1)
    weights = jnp.take(weights, y_src, axis=3)
    weights = weights.transpose(0, 3, 1, 2, 4).reshape(boxes, ny * nx, nz, pool_rows)
    obs_scale = weights * inv_all[None]
    weighted = (obs_scale * innov_all[None]).astype(jnp.bfloat16)
    pad = ((0, 0), (0, 0), (0, 0), (0, block_rows - pool_rows))
    scale_rows = jnp.pad(obs_scale, pad).reshape(boxes, -1)
    scale_rows = jnp.pad(scale_rows, ((0, 8 - boxes), (0, 0)))
    weighted = jnp.pad(weighted, pad).reshape(boxes, -1)
    weighted = jnp.pad(weighted, ((0, 16 - boxes), (0, 0)))
    gram, innov_sum = gram_terms(full.reshape(-1, members), scale_rows, weighted, boxes)
    transform = make_transform(gram, innov_sum)
    smean = jnp.mean(states, axis=2, dtype=jnp.float32)
    state_anomaly = (states.astype(jnp.float32) - smean[:, :, None]).astype(jnp.bfloat16)
    updates = jnp.einsum(
        "fck,bkj->bfcj", state_anomaly, transform, preferred_element_type=jnp.float32
    )
    box_range = jnp.arange(boxes, dtype=jnp.int32)
    selector = (box_ids[None, :] == box_range[:, None]).astype(jnp.float32)
    total = jnp.sum(selector[:, None, :, None] * updates, axis=0)
    return (smean[:, :, None] + total).astype(jnp.bfloat16)


def solution(mesh):
    n_region, n_tile = mesh.devices.shape
    nz = 2
    nx = 4
    ny = n_tile // (nx * nz)
    fine = Mesh(mesh.devices.reshape(n_region, nx, nz, ny), ("region", "tx", "tz", "ty"))
    flat = ("region", "tx", "tz", "ty")
    return jax.shard_map(
        body,
        mesh=fine,
        in_specs=(
            P(flat, None),
            P(flat),
            P(flat),
            P(flat),
            P(flat),
            P(flat, None),
            P(flat, None),
            P(None, flat, None),
            P(flat),
        ),
        out_specs=P(None, flat, None),
        check_vma=False,
    )
```

```python
import functools

import jax
import jax.numpy as jnp
from jax import lax
from jax.experimental import pallas as pl
from jax.experimental.pallas import tpu as pltpu
from jax.sharding import Mesh
from jax.sharding import PartitionSpec as P

HI = lax.Precision.HIGHEST
ROWS_PER_STEP = 1664


def passed_along(block, axis, distance):
    devices = range(lax.axis_size(axis))
    route = [(i - distance, i) for i in devices if i - distance in devices]
    return lax.ppermute(block, axis, route)


def _gram_kernel(a_ref, s_ref, w_ref, g_ref, v_ref):
    @pl.when(pl.program_id(0) == 0)
    def _():
        g_ref[...] = jnp.zeros(g_ref.shape, jnp.float32)
        v_ref[...] = jnp.zeros(v_ref.shape, jnp.float32)

    a = a_ref[...]
    af = a.astype(jnp.float32)
    sv = s_ref[...]
    lanes = 128
    eye = (lax.broadcasted_iota(jnp.int32, (lanes, lanes), 0)
           == lax.broadcasted_iota(jnp.int32, (lanes, lanes), 1))
    for b in range(g_ref.shape[0]):
        cols = [jnp.sum(jnp.where(eye, sv[b:b + 1, c * lanes:(c + 1) * lanes], 0.0),
                        axis=1, keepdims=True)
                for c in range(a.shape[0] // lanes)]
        sc = (af * jnp.concatenate(cols, axis=0)).astype(jnp.bfloat16)
        g_ref[b] += lax.dot_general(sc, a, (((0,), (0,)), ((), ())),
                                    preferred_element_type=jnp.float32)
    v_ref[...] += jnp.dot(w_ref[...], a, preferred_element_type=jnp.float32)


def gram_terms(pool, scale_rows, weighted, gram_boxes):
    rows, members = pool.shape
    boxes = gram_boxes
    srows = scale_rows.shape[0]
    wrows = weighted.shape[0]
    step = ROWS_PER_STEP
    return pl.pallas_call(
        _gram_kernel,
        grid=(rows // step,),
        in_specs=[
            pl.BlockSpec((step, members), lambda i: (i, 0)),
            pl.BlockSpec((srows, step), lambda i: (0, i)),
            pl.BlockSpec((wrows, step), lambda i: (0, i)),
        ],
        out_specs=[
            pl.BlockSpec((boxes, members, members), lambda i: (0, 0, 0)),
            pl.BlockSpec((wrows, members), lambda i: (0, 0)),
        ],
        out_shape=[
            jax.ShapeDtypeStruct((boxes, members, members), jnp.float32),
            jax.ShapeDtypeStruct((wrows, members), jnp.float32),
        ],
    )(pool, scale_rows, weighted)


def _transform_kernel(g_ref, v_ref, t_ref, m_ref, r_ref, *, nb):
    boxes, n, _ = g_ref.shape
    ridx = lax.broadcasted_iota(jnp.int32, (n, n), 0)
    cidx = lax.broadcasted_iota(jnp.int32, (n, n), 1)
    eye = (ridx == cidx).astype(jnp.float32)
    for b in range(boxes):
        m_ref[b] = g_ref[b] + (n - 1.0) * eye
    width = 4
    bi = lax.broadcasted_iota(jnp.int32, (nb, nb), 0)
    bj = lax.broadcasted_iota(jnp.int32, (nb, nb), 1)
    beye = (bi == bj).astype(jnp.float32)

    def mul2(x, y):
        return [[x[i][0] * y[0][j] + x[i][1] * y[1][j] for j in range(2)] for i in range(2)]

    def inv2(x):
        r = 1.0 / (x[0][0] * x[1][1] - x[0][1] * x[1][0])
        return [[x[1][1] * r, -x[0][1] * r], [-x[1][0] * r, x[0][0] * r]]

    def pivot(step, blocks):
        k = width * step
        rmask = [bi == k + m for m in range(width)]
        lmask = [bj[0:1] == k + m for m in range(width)]
        out = []
        for d in blocks:
            rows = [jnp.sum(jnp.where(rmask[m], d, 0.0), axis=0, keepdims=True) for m in range(width)]
            cols = [jnp.sum(jnp.where(bj == k + m, d, 0.0), axis=1, keepdims=True) for m in range(width)]
            p = [[jnp.sum(jnp.where(lmask[j], rows[i], 0.0), axis=1, keepdims=True)
                  for j in range(width)] for i in range(width)]
            a = [[p[0][0], p[0][1]], [p[1][0], p[1][1]]]
            b = [[p[0][2], p[0][3]], [p[1][2], p[1][3]]]
            c = [[p[2][0], p[2][1]], [p[3][0], p[3][1]]]
            e = [[p[2][2], p[2][3]], [p[3][2], p[3][3]]]
            ai = inv2(a)
            aib = mul2(ai, b)
            cai = mul2(c, ai)
            cab = mul2(c, aib)
            si = inv2([[e[i][j] - cab[i][j] for j in range(2)] for i in range(2)])
            q12 = [[-v for v in row] for row in mul2(aib, si)]
            q21 = [[-v for v in row] for row in mul2(si, cai)]
            q12c = mul2(q12, cai)
            q11 = [[ai[i][j] - q12c[i][j] for j in range(2)] for i in range(2)]
            q = [q11[0] + q12[0], q11[1] + q12[1], q21[0] + si[0], q21[1] + si[1]]
            new = d
            gs = []
            for i in range(width):
                rn = q[i][0] * rows[0]
                for j in range(1, width):
                    rn = rn + q[i][j] * rows[j]
                f, g = rn, rn
                for j in range(width):
                    f = jnp.where(lmask[j], q[i][j] + (1.0 if i == j else 0.0), f)
                    g = jnp.where(lmask[j], q[i][j], g)
                new = new - cols[i] * f
                gs.append(g)
            for i in range(width):
                new = jnp.where(rmask[i], gs[i], new)
            out.append(new)
        return tuple(out)

    for kb in range(n // nb):
        s = slice(kb * nb, (kb + 1) * nb)
        dinvs = lax.fori_loop(0, nb // width, pivot, tuple(m_ref[b, s, s] for b in range(boxes)))
        for b in range(boxes):
            dinv = dinvs[b]
            rn = jnp.dot(dinv, m_ref[b, s, :], precision=HI, preferred_element_type=jnp.float32)
            r_ref[b] = rn
            r_ref[b, :, s] = beye + dinv
            upd = jnp.dot(m_ref[b, :, s], r_ref[b], precision=HI, preferred_element_type=jnp.float32)
            m_ref[b] = m_ref[b] - upd
            m_ref[b, s, :] = rn
            m_ref[b, s, s] = dinv
    for b in range(boxes):
        inv = m_ref[b]
        wbar = jnp.sum(inv * v_ref[b:b + 1, :], axis=1, keepdims=True)
        t_ref[b] = (0.5 * eye + (0.5 * (n - 1.0)) * inv + wbar).astype(t_ref.dtype)


def make_transform(gram, innov_rows, nb=64):
    boxes, n, _ = gram.shape
    return pl.pallas_call(
        functools.partial(_transform_kernel, nb=nb),
        out_shape=jax.ShapeDtypeStruct((boxes, n, n), jnp.bfloat16),
        scratch_shapes=[pltpu.VMEM((boxes, n, n), jnp.float32),
                        pltpu.VMEM((boxes, nb, n), jnp.float32)],
    )(gram, innov_rows)


def body(ens_obs, obs_values, obs_var, edge_up, edge_down, loc_local, loc_edge, states, box_ids):
    record_count, members = ens_obs.shape
    nx, nz, ny = lax.axis_size("tx"), lax.axis_size("tz"), lax.axis_size("ty")
    boxes = loc_local.shape[0]
    ymean = jnp.mean(ens_obs, axis=1, dtype=jnp.float32)
    anomaly = (ens_obs.astype(jnp.float32) - ymean[:, None]).astype(jnp.bfloat16)
    inv_var = (1.0 / obs_var).astype(jnp.bfloat16)
    innov = (obs_values - ymean).astype(jnp.bfloat16)
    def edge_payload(index):
        info = jnp.concatenate([inv_var[index], innov[index]])
        info = jnp.pad(info, (0, members - info.shape[0]))
        return jnp.concatenate([anomaly[index], info[None]], axis=0)

    lower = passed_along(edge_payload(edge_up), "region", 1)
    upper = passed_along(edge_payload(edge_down), "region", -1)
    edge = edge_up.shape[0]
    lower_a, lower_v, lower_i = lower[:edge], lower[edge, :edge], lower[edge, edge:2 * edge]
    upper_a, upper_v, upper_i = upper[:edge], upper[edge, :edge], upper[edge, edge:2 * edge]
    edge_rows = lower_a.shape[0] + upper_a.shape[0]
    pool_rows = record_count + edge_rows
    block_rows = ((pool_rows + 1 + 15) // 16) * 16
    info_row = jnp.concatenate(
        [inv_var, lower_v, upper_v, innov, lower_i, upper_i,
         jnp.zeros((members - 2 * pool_rows,), jnp.bfloat16)])
    block = jnp.concatenate(
        [anomaly, lower_a, upper_a, info_row[None],
         jnp.zeros((block_rows - pool_rows - 1, members), jnp.bfloat16)], axis=0)
    half = lax.all_gather(block, "tz", axis=0)
    full = lax.all_gather(half, ("tx", "ty"), axis=0)
    info = full[:, :, pool_rows, :2 * pool_rows].astype(jnp.float32)
    inv_all = info[:, :, :pool_rows]
    innov_all = info[:, :, pool_rows:]
    local_w = loc_local.reshape(boxes, nx, nz, ny, record_count)
    edge_w = loc_edge.reshape(boxes, nx, nz, ny, edge_rows)
    weights = jnp.concatenate([local_w, edge_w], axis=4).transpose(0, 1, 3, 2, 4)
    weights = weights.reshape(boxes, nx * ny, nz, pool_rows)
    obs_scale = weights * inv_all[None]
    weighted = (obs_scale * innov_all[None]).astype(jnp.bfloat16)
    pad = ((0, 0), (0, 0), (0, 0), (0, block_rows - pool_rows))
    scale_rows = jnp.pad(obs_scale, pad).reshape(boxes, -1)
    scale_rows = jnp.pad(scale_rows, ((0, 8 - boxes), (0, 0)))
    weighted = jnp.pad(weighted, pad).reshape(boxes, -1)
    weighted = jnp.pad(weighted, ((0, 16 - boxes), (0, 0)))
    gram, innov_sum = gram_terms(full.reshape(-1, members), scale_rows, weighted, boxes)
    transform = make_transform(gram, innov_sum)
    smean = jnp.mean(states, axis=2, dtype=jnp.float32)
    state_anomaly = (states.astype(jnp.float32) - smean[:, :, None]).astype(jnp.bfloat16)
    updates = jnp.einsum(
        "fck,bkj->bfcj", state_anomaly, transform, preferred_element_type=jnp.float32
    )
    box_range = jnp.arange(boxes, dtype=jnp.int32)
    selector = (box_ids[None, :] == box_range[:, None]).astype(jnp.float32)
    total = jnp.sum(selector[:, None, :, None] * updates, axis=0)
    return (smean[:, :, None] + total).astype(jnp.bfloat16)


def solution(mesh):
    n_region, n_tile = mesh.devices.shape
    nz = 2
    nx = 4
    ny = n_tile // (nx * nz)
    fine = Mesh(mesh.devices.reshape(n_region, nx, nz, ny), ("region", "tx", "tz", "ty"))
    flat = ("region", "tx", "tz", "ty")
    return jax.shard_map(
        body,
        mesh=fine,
        in_specs=(
            P(flat, None),
            P(flat),
            P(flat),
            P(flat),
            P(flat),
            P(flat, None),
            P(flat, None),
            P(None, flat, None),
            P(flat),
        ),
        out_specs=P(None, flat, None),
        check_vma=False,
    )
```

```python
import functools

import jax
import jax.numpy as jnp
from jax import lax
from jax.experimental import pallas as pl
from jax.experimental.pallas import tpu as pltpu
from jax.sharding import Mesh
from jax.sharding import PartitionSpec as P

HI = lax.Precision.HIGHEST
ROWS_PER_STEP = 1664


def passed_along(block, axis, distance):
    devices = range(lax.axis_size(axis))
    route = [(i - distance, i) for i in devices if i - distance in devices]
    return lax.ppermute(block, axis, route)


def _gram_kernel(a_ref, s_ref, w_ref, g_ref, v_ref):
    @pl.when(pl.program_id(0) == 0)
    def _():
        g_ref[...] = jnp.zeros(g_ref.shape, jnp.float32)
        v_ref[...] = jnp.zeros(v_ref.shape, jnp.float32)

    a = a_ref[...]
    af = a.astype(jnp.float32)
    sv = s_ref[...]
    lanes = 128
    eye = (lax.broadcasted_iota(jnp.int32, (lanes, lanes), 0)
           == lax.broadcasted_iota(jnp.int32, (lanes, lanes), 1))
    for b in range(g_ref.shape[0]):
        cols = [jnp.sum(jnp.where(eye, sv[b:b + 1, c * lanes:(c + 1) * lanes], 0.0),
                        axis=1, keepdims=True)
                for c in range(a.shape[0] // lanes)]
        sc = (af * jnp.concatenate(cols, axis=0)).astype(jnp.bfloat16)
        g_ref[b] += lax.dot_general(sc, a, (((0,), (0,)), ((), ())),
                                    preferred_element_type=jnp.float32)
    v_ref[...] += jnp.dot(w_ref[...], a, preferred_element_type=jnp.float32)


def gram_terms(pool, scale_rows, weighted, gram_boxes):
    rows, members = pool.shape
    boxes = gram_boxes
    srows = scale_rows.shape[0]
    wrows = weighted.shape[0]
    step = ROWS_PER_STEP
    return pl.pallas_call(
        _gram_kernel,
        grid=(rows // step,),
        in_specs=[
            pl.BlockSpec((step, members), lambda i: (i, 0)),
            pl.BlockSpec((srows, step), lambda i: (0, i)),
            pl.BlockSpec((wrows, step), lambda i: (0, i)),
        ],
        out_specs=[
            pl.BlockSpec((boxes, members, members), lambda i: (0, 0, 0)),
            pl.BlockSpec((wrows, members), lambda i: (0, 0)),
        ],
        out_shape=[
            jax.ShapeDtypeStruct((boxes, members, members), jnp.float32),
            jax.ShapeDtypeStruct((wrows, members), jnp.float32),
        ],
    )(pool, scale_rows, weighted)


def _transform_kernel(g_ref, v_ref, t_ref, m_ref, r_ref, *, nb):
    boxes, n, _ = g_ref.shape
    ridx = lax.broadcasted_iota(jnp.int32, (n, n), 0)
    cidx = lax.broadcasted_iota(jnp.int32, (n, n), 1)
    eye = (ridx == cidx).astype(jnp.float32)
    for b in range(boxes):
        m_ref[b] = g_ref[b] + (n - 1.0) * eye
    width = 4
    bi = lax.broadcasted_iota(jnp.int32, (nb, nb), 0)
    bj = lax.broadcasted_iota(jnp.int32, (nb, nb), 1)
    beye = (bi == bj).astype(jnp.float32)

    def mul2(x, y):
        return [[x[i][0] * y[0][j] + x[i][1] * y[1][j] for j in range(2)] for i in range(2)]

    def inv2(x):
        r = 1.0 / (x[0][0] * x[1][1] - x[0][1] * x[1][0])
        return [[x[1][1] * r, -x[0][1] * r], [-x[1][0] * r, x[0][0] * r]]

    def pivot(step, blocks):
        k = width * step
        rmask = [bi == k + m for m in range(width)]
        lmask = [bj[0:1] == k + m for m in range(width)]
        out = []
        for d in blocks:
            rows = [jnp.sum(jnp.where(rmask[m], d, 0.0), axis=0, keepdims=True) for m in range(width)]
            cols = [jnp.sum(jnp.where(bj == k + m, d, 0.0), axis=1, keepdims=True) for m in range(width)]
            p = [[jnp.sum(jnp.where(lmask[j], rows[i], 0.0), axis=1, keepdims=True)
                  for j in range(width)] for i in range(width)]
            a = [[p[0][0], p[0][1]], [p[1][0], p[1][1]]]
            b = [[p[0][2], p[0][3]], [p[1][2], p[1][3]]]
            c = [[p[2][0], p[2][1]], [p[3][0], p[3][1]]]
            e = [[p[2][2], p[2][3]], [p[3][2], p[3][3]]]
            ai = inv2(a)
            aib = mul2(ai, b)
            cai = mul2(c, ai)
            cab = mul2(c, aib)
            si = inv2([[e[i][j] - cab[i][j] for j in range(2)] for i in range(2)])
            q12 = [[-v for v in row] for row in mul2(aib, si)]
            q21 = [[-v for v in row] for row in mul2(si, cai)]
            q12c = mul2(q12, cai)
            q11 = [[ai[i][j] - q12c[i][j] for j in range(2)] for i in range(2)]
            q = [q11[0] + q12[0], q11[1] + q12[1], q21[0] + si[0], q21[1] + si[1]]
            new = d
            gs = []
            for i in range(width):
                rn = q[i][0] * rows[0]
                for j in range(1, width):
                    rn = rn + q[i][j] * rows[j]
                f, g = rn, rn
                for j in range(width):
                    f = jnp.where(lmask[j], q[i][j] + (1.0 if i == j else 0.0), f)
                    g = jnp.where(lmask[j], q[i][j], g)
                new = new - cols[i] * f
                gs.append(g)
            for i in range(width):
                new = jnp.where(rmask[i], gs[i], new)
            out.append(new)
        return tuple(out)

    for kb in range(n // nb):
        s = slice(kb * nb, (kb + 1) * nb)
        dinvs = lax.fori_loop(0, nb // width, pivot, tuple(m_ref[b, s, s] for b in range(boxes)))
        for b in range(boxes):
            dinv = dinvs[b]
            rn = jnp.dot(dinv, m_ref[b, s, :], precision=HI, preferred_element_type=jnp.float32)
            r_ref[b] = rn
            r_ref[b, :, s] = beye + dinv
            upd = jnp.dot(m_ref[b, :, s], r_ref[b], precision=HI, preferred_element_type=jnp.float32)
            m_ref[b] = m_ref[b] - upd
            m_ref[b, s, :] = rn
            m_ref[b, s, s] = dinv
    for b in range(boxes):
        inv = m_ref[b]
        wbar = jnp.sum(inv * v_ref[b:b + 1, :], axis=1, keepdims=True)
        t_ref[b] = (0.5 * eye + (0.5 * (n - 1.0)) * inv + wbar).astype(t_ref.dtype)


def make_transform(gram, innov_rows, nb=64):
    boxes, n, _ = gram.shape
    return pl.pallas_call(
        functools.partial(_transform_kernel, nb=nb),
        out_shape=jax.ShapeDtypeStruct((boxes, n, n), jnp.bfloat16),
        scratch_shapes=[pltpu.VMEM((boxes, n, n), jnp.float32),
                        pltpu.VMEM((boxes, nb, n), jnp.float32)],
    )(gram, innov_rows)


def body(ens_obs, obs_values, obs_var, edge_up, edge_down, loc_local, loc_edge, states, box_ids):
    record_count, members = ens_obs.shape
    nx, nz, ny = lax.axis_size("tx"), lax.axis_size("tz"), lax.axis_size("ty")
    boxes = loc_local.shape[0]
    ymean = jnp.mean(ens_obs, axis=1, dtype=jnp.float32)
    anomaly = (ens_obs.astype(jnp.float32) - ymean[:, None]).astype(jnp.bfloat16)
    inv_var = (1.0 / obs_var).astype(jnp.bfloat16)
    innov = (obs_values - ymean).astype(jnp.bfloat16)
    def edge_payload(index):
        info = jnp.concatenate([inv_var[index], innov[index]])
        info = jnp.pad(info, (0, members - info.shape[0]))
        return jnp.concatenate([anomaly[index], info[None]], axis=0)

    lower = passed_along(edge_payload(edge_up), "region", 1)
    upper = passed_along(edge_payload(edge_down), "region", -1)
    edge = edge_up.shape[0]
    lower_a, lower_v, lower_i = lower[:edge], lower[edge, :edge], lower[edge, edge:2 * edge]
    upper_a, upper_v, upper_i = upper[:edge], upper[edge, :edge], upper[edge, edge:2 * edge]
    edge_rows = lower_a.shape[0] + upper_a.shape[0]
    pool_rows = record_count + edge_rows
    block_rows = ((pool_rows + 1 + 15) // 16) * 16
    info_row = jnp.concatenate(
        [inv_var, lower_v, upper_v, innov, lower_i, upper_i,
         jnp.zeros((members - 2 * pool_rows,), jnp.bfloat16)])
    block = jnp.concatenate(
        [anomaly, lower_a, upper_a, info_row[None],
         jnp.zeros((block_rows - pool_rows - 1, members), jnp.bfloat16)], axis=0)
    half = lax.all_gather(block, "tz", axis=0)
    plane = nx * ny
    spread = jnp.broadcast_to(half[None], (plane,) + half.shape).reshape((plane * nz,) + half.shape[1:])
    full = lax.all_to_all(spread, ("tx", "ty"), 0, 0, tiled=True).reshape((plane,) + half.shape)
    info = full[:, :, pool_rows, :2 * pool_rows].astype(jnp.float32)
    inv_all = info[:, :, :pool_rows]
    innov_all = info[:, :, pool_rows:]
    local_w = loc_local.reshape(boxes, nx, nz, ny, record_count)
    edge_w = loc_edge.reshape(boxes, nx, nz, ny, edge_rows)
    weights = jnp.concatenate([local_w, edge_w], axis=4).transpose(0, 1, 3, 2, 4)
    weights = weights.reshape(boxes, nx * ny, nz, pool_rows)
    obs_scale = weights * inv_all[None]
    weighted = (obs_scale * innov_all[None]).astype(jnp.bfloat16)
    pad = ((0, 0), (0, 0), (0, 0), (0, block_rows - pool_rows))
    scale_rows = jnp.pad(obs_scale, pad).reshape(boxes, -1)
    scale_rows = jnp.pad(scale_rows, ((0, 8 - boxes), (0, 0)))
    weighted = jnp.pad(weighted, pad).reshape(boxes, -1)
    weighted = jnp.pad(weighted, ((0, 16 - boxes), (0, 0)))
    gram, innov_sum = gram_terms(full.reshape(-1, members), scale_rows, weighted, boxes)
    transform = make_transform(gram, innov_sum)
    smean = jnp.mean(states, axis=2, dtype=jnp.float32)
    state_anomaly = (states.astype(jnp.float32) - smean[:, :, None]).astype(jnp.bfloat16)
    updates = jnp.einsum(
        "fck,bkj->bfcj", state_anomaly, transform, preferred_element_type=jnp.float32
    )
    box_range = jnp.arange(boxes, dtype=jnp.int32)
    selector = (box_ids[None, :] == box_range[:, None]).astype(jnp.float32)
    total = jnp.sum(selector[:, None, :, None] * updates, axis=0)
    return (smean[:, :, None] + total).astype(jnp.bfloat16)


def solution(mesh):
    n_region, n_tile = mesh.devices.shape
    nz = 2
    nx = 4
    ny = n_tile // (nx * nz)
    fine = Mesh(mesh.devices.reshape(n_region, nx, nz, ny), ("region", "tx", "tz", "ty"))
    flat = ("region", "tx", "tz", "ty")
    return jax.shard_map(
        body,
        mesh=fine,
        in_specs=(
            P(flat, None),
            P(flat),
            P(flat),
            P(flat),
            P(flat),
            P(flat, None),
            P(flat, None),
            P(None, flat, None),
            P(flat),
        ),
        out_specs=P(None, flat, None),
        check_vma=False,
    )
```

```python
import functools

import jax
import jax.numpy as jnp
from jax import lax
from jax.experimental import pallas as pl
from jax.experimental.pallas import tpu as pltpu
from jax.sharding import Mesh
from jax.sharding import PartitionSpec as P

HI = lax.Precision.HIGHEST
ROWS_PER_STEP = 3328


def passed_along(block, axis, distance):
    devices = range(lax.axis_size(axis))
    route = [(i - distance, i) for i in devices if i - distance in devices]
    return lax.ppermute(block, axis, route)


def _gram_kernel(a_ref, s_ref, w_ref, g_ref, v_ref):
    @pl.when(pl.program_id(0) == 0)
    def _():
        g_ref[...] = jnp.zeros(g_ref.shape, jnp.float32)
        v_ref[...] = jnp.zeros(v_ref.shape, jnp.float32)

    a = a_ref[...]
    at = a.astype(jnp.float32).T
    for b in range(g_ref.shape[0]):
        sct = (at * s_ref[b:b + 1, :]).astype(jnp.bfloat16)
        g_ref[b] += jnp.dot(sct, a, preferred_element_type=jnp.float32)
    v_ref[...] += jnp.dot(w_ref[...], a, preferred_element_type=jnp.float32)


def gram_terms(pool, scale_rows, weighted, gram_boxes):
    rows, members = pool.shape
    boxes = gram_boxes
    srows = scale_rows.shape[0]
    wrows = weighted.shape[0]
    step = ROWS_PER_STEP
    return pl.pallas_call(
        _gram_kernel,
        grid=(rows // step,),
        in_specs=[
            pl.BlockSpec((step, members), lambda i: (i, 0)),
            pl.BlockSpec((srows, step), lambda i: (0, i)),
            pl.BlockSpec((wrows, step), lambda i: (0, i)),
        ],
        out_specs=[
            pl.BlockSpec((boxes, members, members), lambda i: (0, 0, 0)),
            pl.BlockSpec((wrows, members), lambda i: (0, 0)),
        ],
        out_shape=[
            jax.ShapeDtypeStruct((boxes, members, members), jnp.float32),
            jax.ShapeDtypeStruct((wrows, members), jnp.float32),
        ],
    )(pool, scale_rows, weighted)


def _transform_kernel(g_ref, v_ref, t_ref, m_ref, r_ref, *, nb):
    boxes, n, _ = g_ref.shape
    ridx = lax.broadcasted_iota(jnp.int32, (n, n), 0)
    cidx = lax.broadcasted_iota(jnp.int32, (n, n), 1)
    eye = (ridx == cidx).astype(jnp.float32)
    for b in range(boxes):
        m_ref[b] = g_ref[b] + (n - 1.0) * eye
    width = 4
    bi = lax.broadcasted_iota(jnp.int32, (nb, nb), 0)
    bj = lax.broadcasted_iota(jnp.int32, (nb, nb), 1)
    beye = (bi == bj).astype(jnp.float32)

    def mul2(x, y):
        return [[x[i][0] * y[0][j] + x[i][1] * y[1][j] for j in range(2)] for i in range(2)]

    def inv2(x):
        r = 1.0 / (x[0][0] * x[1][1] - x[0][1] * x[1][0])
        return [[x[1][1] * r, -x[0][1] * r], [-x[1][0] * r, x[0][0] * r]]

    def pivot(step, blocks):
        k = width * step
        rmask = [bi == k + m for m in range(width)]
        lmask = [bj[0:1] == k + m for m in range(width)]
        out = []
        for d in blocks:
            rows = [jnp.sum(jnp.where(rmask[m], d, 0.0), axis=0, keepdims=True) for m in range(width)]
            cols = [jnp.sum(jnp.where(bj == k + m, d, 0.0), axis=1, keepdims=True) for m in range(width)]
            p = [[jnp.sum(jnp.where(lmask[j], rows[i], 0.0), axis=1, keepdims=True)
                  for j in range(width)] for i in range(width)]
            a = [[p[0][0], p[0][1]], [p[1][0], p[1][1]]]
            b = [[p[0][2], p[0][3]], [p[1][2], p[1][3]]]
            c = [[p[2][0], p[2][1]], [p[3][0], p[3][1]]]
            e = [[p[2][2], p[2][3]], [p[3][2], p[3][3]]]
            ai = inv2(a)
            aib = mul2(ai, b)
            cai = mul2(c, ai)
            cab = mul2(c, aib)
            si = inv2([[e[i][j] - cab[i][j] for j in range(2)] for i in range(2)])
            q12 = [[-v for v in row] for row in mul2(aib, si)]
            q21 = [[-v for v in row] for row in mul2(si, cai)]
            q12c = mul2(q12, cai)
            q11 = [[ai[i][j] - q12c[i][j] for j in range(2)] for i in range(2)]
            q = [q11[0] + q12[0], q11[1] + q12[1], q21[0] + si[0], q21[1] + si[1]]
            new = d
            gs = []
            for i in range(width):
                rn = q[i][0] * rows[0]
                for j in range(1, width):
                    rn = rn + q[i][j] * rows[j]
                f, g = rn, rn
                for j in range(width):
                    f = jnp.where(lmask[j], q[i][j] + (1.0 if i == j else 0.0), f)
                    g = jnp.where(lmask[j], q[i][j], g)
                new = new - cols[i] * f
                gs.append(g)
            for i in range(width):
                new = jnp.where(rmask[i], gs[i], new)
            out.append(new)
        return tuple(out)

    for kb in range(n // nb):
        s = slice(kb * nb, (kb + 1) * nb)
        dinvs = lax.fori_loop(0, nb // width, pivot, tuple(m_ref[b, s, s] for b in range(boxes)))
        for b in range(boxes):
            dinv = dinvs[b]
            rn = jnp.dot(dinv, m_ref[b, s, :], precision=HI, preferred_element_type=jnp.float32)
            r_ref[b] = rn
            r_ref[b, :, s] = beye + dinv
            upd = jnp.dot(m_ref[b, :, s], r_ref[b], precision=HI, preferred_element_type=jnp.float32)
            m_ref[b] = m_ref[b] - upd
            m_ref[b, s, :] = rn
            m_ref[b, s, s] = dinv
    for b in range(boxes):
        inv = m_ref[b]
        wbar = jnp.sum(inv * v_ref[b:b + 1, :], axis=1, keepdims=True)
        t_ref[b] = (0.5 * eye + (0.5 * (n - 1.0)) * inv + wbar).astype(t_ref.dtype)


def make_transform(gram, innov_rows, nb=64):
    boxes, n, _ = gram.shape
    return pl.pallas_call(
        functools.partial(_transform_kernel, nb=nb),
        out_shape=jax.ShapeDtypeStruct((boxes, n, n), jnp.bfloat16),
        scratch_shapes=[pltpu.VMEM((boxes, n, n), jnp.float32),
                        pltpu.VMEM((boxes, nb, n), jnp.float32)],
    )(gram, innov_rows)


def body(ens_obs, obs_values, obs_var, edge_up, edge_down, loc_local, loc_edge, states, box_ids):
    record_count, members = ens_obs.shape
    nx, nz, ny = lax.axis_size("tx"), lax.axis_size("tz"), lax.axis_size("ty")
    boxes = loc_local.shape[0]
    ymean = jnp.mean(ens_obs, axis=1, dtype=jnp.float32)
    anomaly = (ens_obs.astype(jnp.float32) - ymean[:, None]).astype(jnp.bfloat16)
    inv_var = (1.0 / obs_var).astype(jnp.bfloat16)
    innov = (obs_values - ymean).astype(jnp.bfloat16)
    def edge_payload(index):
        info = jnp.concatenate([inv_var[index], innov[index]])
        info = jnp.pad(info, (0, members - info.shape[0]))
        return jnp.concatenate([anomaly[index], info[None]], axis=0)

    lower = passed_along(edge_payload(edge_up), "region", 1)
    upper = passed_along(edge_payload(edge_down), "region", -1)
    edge = edge_up.shape[0]
    lower_a, lower_v, lower_i = lower[:edge], lower[edge, :edge], lower[edge, edge:2 * edge]
    upper_a, upper_v, upper_i = upper[:edge], upper[edge, :edge], upper[edge, edge:2 * edge]
    edge_rows = lower_a.shape[0] + upper_a.shape[0]
    pool_rows = record_count + edge_rows
    block_rows = ((pool_rows + 1 + 15) // 16) * 16
    info_row = jnp.concatenate(
        [inv_var, lower_v, upper_v, innov, lower_i, upper_i,
         jnp.zeros((members - 2 * pool_rows,), jnp.bfloat16)])
    block = jnp.concatenate(
        [anomaly, lower_a, upper_a, info_row[None],
         jnp.zeros((block_rows - pool_rows - 1, members), jnp.bfloat16)], axis=0)
    half = lax.all_gather(block, "tz", axis=0)
    full = lax.all_gather(half, ("tx", "ty"), axis=0)
    info = full[:, :, pool_rows, :2 * pool_rows].astype(jnp.float32)
    inv_all = info[:, :, :pool_rows]
    innov_all = info[:, :, pool_rows:]
    local_w = loc_local.reshape(boxes, nx, nz, ny, record_count)
    edge_w = loc_edge.reshape(boxes, nx, nz, ny, edge_rows)
    weights = jnp.concatenate([local_w, edge_w], axis=4).transpose(0, 1, 3, 2, 4)
    weights = weights.reshape(boxes, nx * ny, nz, pool_rows)
    obs_scale = weights * inv_all[None]
    weighted = (obs_scale * innov_all[None]).astype(jnp.bfloat16)
    pad = ((0, 0), (0, 0), (0, 0), (0, block_rows - pool_rows))
    scale_rows = jnp.pad(obs_scale, pad).reshape(boxes, -1)
    scale_rows = jnp.pad(scale_rows, ((0, 8 - boxes), (0, 0)))
    weighted = jnp.pad(weighted, pad).reshape(boxes, -1)
    weighted = jnp.pad(weighted, ((0, 16 - boxes), (0, 0)))
    gram, innov_sum = gram_terms(full.reshape(-1, members), scale_rows, weighted, boxes)
    transform = make_transform(gram, innov_sum)
    smean = jnp.mean(states, axis=2, dtype=jnp.float32)
    state_anomaly = (states.astype(jnp.float32) - smean[:, :, None]).astype(jnp.bfloat16)
    updates = jnp.einsum(
        "fck,bkj->bfcj", state_anomaly, transform, preferred_element_type=jnp.float32
    )
    box_range = jnp.arange(boxes, dtype=jnp.int32)
    selector = (box_ids[None, :] == box_range[:, None]).astype(jnp.float32)
    total = jnp.sum(selector[:, None, :, None] * updates, axis=0)
    return (smean[:, :, None] + total).astype(jnp.bfloat16)


def solution(mesh):
    n_region, n_tile = mesh.devices.shape
    nz = 2
    nx = 4
    ny = n_tile // (nx * nz)
    fine = Mesh(mesh.devices.reshape(n_region, nx, nz, ny), ("region", "tx", "tz", "ty"))
    flat = ("region", "tx", "tz", "ty")
    return jax.shard_map(
        body,
        mesh=fine,
        in_specs=(
            P(flat, None),
            P(flat),
            P(flat),
            P(flat),
            P(flat),
            P(flat, None),
            P(flat, None),
            P(None, flat, None),
            P(flat),
        ),
        out_specs=P(None, flat, None),
        check_vma=False,
    )
```

```python
import functools

import jax
import jax.numpy as jnp
from jax import lax
from jax.experimental import pallas as pl
from jax.experimental.pallas import tpu as pltpu
from jax.sharding import Mesh
from jax.sharding import PartitionSpec as P

HI = lax.Precision.HIGHEST
ROWS_PER_STEP = 3328


def passed_along(block, axis, distance):
    devices = range(lax.axis_size(axis))
    route = [(i - distance, i) for i in devices if i - distance in devices]
    return lax.ppermute(block, axis, route)


def _gram_kernel(a_ref, s_ref, w_ref, g_ref, v_ref):
    @pl.when(pl.program_id(0) == 0)
    def _():
        g_ref[...] = jnp.zeros(g_ref.shape, jnp.float32)
        v_ref[...] = jnp.zeros(v_ref.shape, jnp.float32)

    a = a_ref[...]
    at = a.astype(jnp.float32).T
    for b in range(g_ref.shape[0]):
        sct = (at * s_ref[b:b + 1, :]).astype(jnp.bfloat16)
        g_ref[b] += jnp.dot(sct, a, preferred_element_type=jnp.float32)
    v_ref[...] += jnp.dot(w_ref[...], a, preferred_element_type=jnp.float32)


def gram_terms(pool, scale_rows, weighted, gram_boxes):
    rows, members = pool.shape
    boxes = gram_boxes
    srows = scale_rows.shape[0]
    wrows = weighted.shape[0]
    step = ROWS_PER_STEP
    return pl.pallas_call(
        _gram_kernel,
        grid=(rows // step,),
        in_specs=[
            pl.BlockSpec((step, members), lambda i: (i, 0)),
            pl.BlockSpec((srows, step), lambda i: (0, i)),
            pl.BlockSpec((wrows, step), lambda i: (0, i)),
        ],
        out_specs=[
            pl.BlockSpec((boxes, members, members), lambda i: (0, 0, 0)),
            pl.BlockSpec((wrows, members), lambda i: (0, 0)),
        ],
        out_shape=[
            jax.ShapeDtypeStruct((boxes, members, members), jnp.float32),
            jax.ShapeDtypeStruct((wrows, members), jnp.float32),
        ],
    )(pool, scale_rows, weighted)


def _transform_kernel(g_ref, v_ref, t_ref, m_ref, r_ref, *, nb):
    boxes, n, _ = g_ref.shape
    ridx = lax.broadcasted_iota(jnp.int32, (n, n), 0)
    cidx = lax.broadcasted_iota(jnp.int32, (n, n), 1)
    eye = (ridx == cidx).astype(jnp.float32)
    for b in range(boxes):
        m_ref[b] = g_ref[b] + (n - 1.0) * eye
    width = 4
    bi = lax.broadcasted_iota(jnp.int32, (nb, nb), 0)
    bj = lax.broadcasted_iota(jnp.int32, (nb, nb), 1)
    beye = (bi == bj).astype(jnp.float32)

    def mul2(x, y):
        return [[x[i][0] * y[0][j] + x[i][1] * y[1][j] for j in range(2)] for i in range(2)]

    def inv2(x):
        r = 1.0 / (x[0][0] * x[1][1] - x[0][1] * x[1][0])
        return [[x[1][1] * r, -x[0][1] * r], [-x[1][0] * r, x[0][0] * r]]

    def pivot(step, blocks):
        k = width * step
        rmask = [bi == k + m for m in range(width)]
        lmask = [bj[0:1] == k + m for m in range(width)]
        out = []
        for d in blocks:
            rows = [jnp.sum(jnp.where(rmask[m], d, 0.0), axis=0, keepdims=True) for m in range(width)]
            cols = [jnp.sum(jnp.where(bj == k + m, d, 0.0), axis=1, keepdims=True) for m in range(width)]
            p = [[jnp.sum(jnp.where(lmask[j], rows[i], 0.0), axis=1, keepdims=True)
                  for j in range(width)] for i in range(width)]
            a = [[p[0][0], p[0][1]], [p[1][0], p[1][1]]]
            b = [[p[0][2], p[0][3]], [p[1][2], p[1][3]]]
            c = [[p[2][0], p[2][1]], [p[3][0], p[3][1]]]
            e = [[p[2][2], p[2][3]], [p[3][2], p[3][3]]]
            ai = inv2(a)
            aib = mul2(ai, b)
            cai = mul2(c, ai)
            cab = mul2(c, aib)
            si = inv2([[e[i][j] - cab[i][j] for j in range(2)] for i in range(2)])
            q12 = [[-v for v in row] for row in mul2(aib, si)]
            q21 = [[-v for v in row] for row in mul2(si, cai)]
            q12c = mul2(q12, cai)
            q11 = [[ai[i][j] - q12c[i][j] for j in range(2)] for i in range(2)]
            q = [q11[0] + q12[0], q11[1] + q12[1], q21[0] + si[0], q21[1] + si[1]]
            new = d
            gs = []
            for i in range(width):
                rn = q[i][0] * rows[0]
                for j in range(1, width):
                    rn = rn + q[i][j] * rows[j]
                f, g = rn, rn
                for j in range(width):
                    f = jnp.where(lmask[j], q[i][j] + (1.0 if i == j else 0.0), f)
                    g = jnp.where(lmask[j], q[i][j], g)
                new = new - cols[i] * f
                gs.append(g)
            for i in range(width):
                new = jnp.where(rmask[i], gs[i], new)
            out.append(new)
        return tuple(out)

    for kb in range(n // nb):
        s = slice(kb * nb, (kb + 1) * nb)
        dinvs = lax.fori_loop(0, nb // width, pivot, tuple(m_ref[b, s, s] for b in range(boxes)))
        for b in range(boxes):
            dinv = dinvs[b]
            rn = jnp.dot(dinv, m_ref[b, s, :], precision=HI, preferred_element_type=jnp.float32)
            r_ref[b] = rn
            r_ref[b, :, s] = beye + dinv
            upd = jnp.dot(m_ref[b, :, s], r_ref[b], precision=HI, preferred_element_type=jnp.float32)
            m_ref[b] = m_ref[b] - upd
            m_ref[b, s, :] = rn
            m_ref[b, s, s] = dinv
    for b in range(boxes):
        inv = m_ref[b]
        wbar = jnp.sum(inv * v_ref[b:b + 1, :], axis=1, keepdims=True)
        t_ref[b] = (0.5 * eye + (0.5 * (n - 1.0)) * inv + wbar).astype(t_ref.dtype)


def make_transform(gram, innov_rows, nb=64):
    boxes, n, _ = gram.shape
    return pl.pallas_call(
        functools.partial(_transform_kernel, nb=nb),
        out_shape=jax.ShapeDtypeStruct((boxes, n, n), jnp.bfloat16),
        scratch_shapes=[pltpu.VMEM((boxes, n, n), jnp.float32),
                        pltpu.VMEM((boxes, nb, n), jnp.float32)],
    )(gram, innov_rows)


def body(ens_obs, obs_values, obs_var, edge_up, edge_down, loc_local, loc_edge, states, box_ids):
    record_count, members = ens_obs.shape
    nx, nz, ny = lax.axis_size("tx"), lax.axis_size("tz"), lax.axis_size("ty")
    boxes = loc_local.shape[0]
    ymean = jnp.mean(ens_obs, axis=1, dtype=jnp.float32)
    anomaly = (ens_obs.astype(jnp.float32) - ymean[:, None]).astype(jnp.bfloat16)
    inv_var = (1.0 / obs_var).astype(jnp.bfloat16)
    innov = (obs_values - ymean).astype(jnp.bfloat16)
    def edge_payload(index):
        info = jnp.concatenate([inv_var[index], innov[index]])
        info = jnp.pad(info, (0, members - info.shape[0]))
        return jnp.concatenate([anomaly[index], info[None]], axis=0)

    lower = passed_along(edge_payload(edge_up), "region", 1)
    upper = passed_along(edge_payload(edge_down), "region", -1)
    edge = edge_up.shape[0]
    lower_a, lower_v, lower_i = lower[:edge], lower[edge, :edge], lower[edge, edge:2 * edge]
    upper_a, upper_v, upper_i = upper[:edge], upper[edge, :edge], upper[edge, edge:2 * edge]
    edge_rows = lower_a.shape[0] + upper_a.shape[0]
    pool_rows = record_count + edge_rows
    block_rows = ((pool_rows + 1 + 15) // 16) * 16
    info_row = jnp.concatenate(
        [inv_var, lower_v, upper_v, innov, lower_i, upper_i,
         jnp.zeros((members - 2 * pool_rows,), jnp.bfloat16)])
    block = jnp.concatenate(
        [anomaly, lower_a, upper_a, info_row[None],
         jnp.zeros((block_rows - pool_rows - 1, members), jnp.bfloat16)], axis=0)
    half = jnp.stack([block, lax.ppermute(block, "tz", [(0, 1), (1, 0)])])
    full = lax.all_gather(half, ("tx", "ty"), axis=0)
    info = full[:, :, pool_rows, :2 * pool_rows].astype(jnp.float32)
    inv_all = info[:, :, :pool_rows]
    innov_all = info[:, :, pool_rows:]
    local_w = loc_local.reshape(boxes, nx, nz, ny, record_count)
    edge_w = loc_edge.reshape(boxes, nx, nz, ny, edge_rows)
    weights = jnp.concatenate([local_w, edge_w], axis=4)
    weights = jnp.take(weights, (lax.axis_index("tz") + jnp.arange(nz)) % nz, axis=2)
    weights = weights.transpose(0, 1, 3, 2, 4)
    weights = weights.reshape(boxes, nx * ny, nz, pool_rows)
    obs_scale = weights * inv_all[None]
    weighted = (obs_scale * innov_all[None]).astype(jnp.bfloat16)
    pad = ((0, 0), (0, 0), (0, 0), (0, block_rows - pool_rows))
    scale_rows = jnp.pad(obs_scale, pad).reshape(boxes, -1)
    scale_rows = jnp.pad(scale_rows, ((0, 8 - boxes), (0, 0)))
    weighted = jnp.pad(weighted, pad).reshape(boxes, -1)
    weighted = jnp.pad(weighted, ((0, 16 - boxes), (0, 0)))
    gram, innov_sum = gram_terms(full.reshape(-1, members), scale_rows, weighted, boxes)
    transform = make_transform(gram, innov_sum)
    smean = jnp.mean(states, axis=2, dtype=jnp.float32)
    state_anomaly = (states.astype(jnp.float32) - smean[:, :, None]).astype(jnp.bfloat16)
    updates = jnp.einsum(
        "fck,bkj->bfcj", state_anomaly, transform, preferred_element_type=jnp.float32
    )
    box_range = jnp.arange(boxes, dtype=jnp.int32)
    selector = (box_ids[None, :] == box_range[:, None]).astype(jnp.float32)
    total = jnp.sum(selector[:, None, :, None] * updates, axis=0)
    return (smean[:, :, None] + total).astype(jnp.bfloat16)


def solution(mesh):
    n_region, n_tile = mesh.devices.shape
    nz = 2
    nx = 4
    ny = n_tile // (nx * nz)
    fine = Mesh(mesh.devices.reshape(n_region, nx, nz, ny), ("region", "tx", "tz", "ty"))
    flat = ("region", "tx", "tz", "ty")
    return jax.shard_map(
        body,
        mesh=fine,
        in_specs=(
            P(flat, None),
            P(flat),
            P(flat),
            P(flat),
            P(flat),
            P(flat, None),
            P(flat, None),
            P(None, flat, None),
            P(flat),
        ),
        out_specs=P(None, flat, None),
        check_vma=False,
    )
```

```python
import functools

import jax
import jax.numpy as jnp
from jax import lax
from jax.experimental import pallas as pl
from jax.experimental.pallas import tpu as pltpu
from jax.sharding import Mesh
from jax.sharding import PartitionSpec as P

HI = lax.Precision.HIGHEST
ROWS_PER_STEP = 3328


def passed_along(block, axis, distance):
    devices = range(lax.axis_size(axis))
    route = [(i - distance, i) for i in devices if i - distance in devices]
    return lax.ppermute(block, axis, route)


def _gram_kernel(a_ref, s_ref, w_ref, g_ref, v_ref):
    @pl.when(pl.program_id(0) == 0)
    def _():
        g_ref[...] = jnp.zeros(g_ref.shape, jnp.float32)
        v_ref[...] = jnp.zeros(v_ref.shape, jnp.float32)

    a = a_ref[...]
    at = a.astype(jnp.float32).T
    for b in range(g_ref.shape[0]):
        sct = (at * s_ref[b:b + 1, :]).astype(jnp.bfloat16)
        g_ref[b] += jnp.dot(sct, a, preferred_element_type=jnp.float32)
    v_ref[...] += jnp.dot(w_ref[...], a, preferred_element_type=jnp.float32)


def gram_terms(pool, scale_rows, weighted, gram_boxes):
    rows, members = pool.shape
    boxes = gram_boxes
    srows = scale_rows.shape[0]
    wrows = weighted.shape[0]
    step = ROWS_PER_STEP
    return pl.pallas_call(
        _gram_kernel,
        grid=(rows // step,),
        in_specs=[
            pl.BlockSpec((step, members), lambda i: (i, 0)),
            pl.BlockSpec((srows, step), lambda i: (0, i)),
            pl.BlockSpec((wrows, step), lambda i: (0, i)),
        ],
        out_specs=[
            pl.BlockSpec((boxes, members, members), lambda i: (0, 0, 0)),
            pl.BlockSpec((wrows, members), lambda i: (0, 0)),
        ],
        out_shape=[
            jax.ShapeDtypeStruct((boxes, members, members), jnp.float32),
            jax.ShapeDtypeStruct((wrows, members), jnp.float32),
        ],
    )(pool, scale_rows, weighted)


def _transform_kernel(g_ref, v_ref, s_ref, box_ref, o_ref, t_ref, m_ref, r_ref, *, nb):
    boxes, n, _ = g_ref.shape
    ridx = lax.broadcasted_iota(jnp.int32, (n, n), 0)
    cidx = lax.broadcasted_iota(jnp.int32, (n, n), 1)
    eye = (ridx == cidx).astype(jnp.float32)
    for b in range(boxes):
        m_ref[b] = g_ref[b] + (n - 1.0) * eye
    width = 4
    bi = lax.broadcasted_iota(jnp.int32, (nb, nb), 0)
    bj = lax.broadcasted_iota(jnp.int32, (nb, nb), 1)
    beye = (bi == bj).astype(jnp.float32)

    def mul2(x, y):
        return [[x[i][0] * y[0][j] + x[i][1] * y[1][j] for j in range(2)] for i in range(2)]

    def inv2(x):
        r = 1.0 / (x[0][0] * x[1][1] - x[0][1] * x[1][0])
        return [[x[1][1] * r, -x[0][1] * r], [-x[1][0] * r, x[0][0] * r]]

    def pivot(step, blocks):
        k = width * step
        rmask = [bi == k + m for m in range(width)]
        lmask = [bj[0:1] == k + m for m in range(width)]
        out = []
        for d in blocks:
            rows = [jnp.sum(jnp.where(rmask[m], d, 0.0), axis=0, keepdims=True) for m in range(width)]
            cols = [jnp.sum(jnp.where(bj == k + m, d, 0.0), axis=1, keepdims=True) for m in range(width)]
            p = [[jnp.sum(jnp.where(lmask[j], rows[i], 0.0), axis=1, keepdims=True)
                  for j in range(width)] for i in range(width)]
            a = [[p[0][0], p[0][1]], [p[1][0], p[1][1]]]
            b = [[p[0][2], p[0][3]], [p[1][2], p[1][3]]]
            c = [[p[2][0], p[2][1]], [p[3][0], p[3][1]]]
            e = [[p[2][2], p[2][3]], [p[3][2], p[3][3]]]
            ai = inv2(a)
            aib = mul2(ai, b)
            cai = mul2(c, ai)
            cab = mul2(c, aib)
            si = inv2([[e[i][j] - cab[i][j] for j in range(2)] for i in range(2)])
            q12 = [[-v for v in row] for row in mul2(aib, si)]
            q21 = [[-v for v in row] for row in mul2(si, cai)]
            q12c = mul2(q12, cai)
            q11 = [[ai[i][j] - q12c[i][j] for j in range(2)] for i in range(2)]
            q = [q11[0] + q12[0], q11[1] + q12[1], q21[0] + si[0], q21[1] + si[1]]
            new = d
            gs = []
            for i in range(width):
                rn = q[i][0] * rows[0]
                for j in range(1, width):
                    rn = rn + q[i][j] * rows[j]
                f, g = rn, rn
                for j in range(width):
                    f = jnp.where(lmask[j], q[i][j] + (1.0 if i == j else 0.0), f)
                    g = jnp.where(lmask[j], q[i][j], g)
                new = new - cols[i] * f
                gs.append(g)
            for i in range(width):
                new = jnp.where(rmask[i], gs[i], new)
            out.append(new)
        return tuple(out)

    for kb in range(n // nb):
        s = slice(kb * nb, (kb + 1) * nb)
        dinvs = lax.fori_loop(0, nb // width, pivot, tuple(m_ref[b, s, s] for b in range(boxes)))
        for b in range(boxes):
            dinv = dinvs[b]
            rn = jnp.dot(dinv, m_ref[b, s, :], precision=HI, preferred_element_type=jnp.float32)
            r_ref[b] = rn
            r_ref[b, :, s] = beye + dinv
            upd = jnp.dot(m_ref[b, :, s], r_ref[b], precision=HI, preferred_element_type=jnp.float32)
            m_ref[b] = m_ref[b] - upd
            m_ref[b, s, :] = rn
            m_ref[b, s, s] = dinv
    for b in range(boxes):
        inv = m_ref[b]
        wbar = jnp.sum(inv * v_ref[b:b + 1, :], axis=1, keepdims=True)
        t_ref[b] = (0.5 * eye + (0.5 * (n - 1.0)) * inv + wbar).astype(t_ref.dtype)
    box = box_ref[...]
    for f in range(s_ref.shape[0]):
        wide = s_ref[f].astype(jnp.float32)
        smean = jnp.sum(wide, axis=1, keepdims=True) / n
        anomaly = (wide - smean).astype(jnp.bfloat16)
        total = jnp.zeros(wide.shape, jnp.float32)
        for b in range(boxes):
            upd = jnp.dot(anomaly, t_ref[b], preferred_element_type=jnp.float32)
            total = total + jnp.where(box == b, upd, 0.0)
        o_ref[f] = (smean + total).astype(o_ref.dtype)


def analysis_of(gram, innov_rows, states, box_col, nb=64):
    boxes, n, _ = gram.shape
    return pl.pallas_call(
        functools.partial(_transform_kernel, nb=nb),
        out_shape=jax.ShapeDtypeStruct(states.shape, states.dtype),
        scratch_shapes=[pltpu.VMEM((boxes, n, n), jnp.bfloat16),
                        pltpu.VMEM((boxes, n, n), jnp.float32),
                        pltpu.VMEM((boxes, nb, n), jnp.float32)],
    )(gram, innov_rows, states, box_col)


def body(ens_obs, obs_values, obs_var, edge_up, edge_down, loc_local, loc_edge, states, box_ids):
    record_count, members = ens_obs.shape
    nx, nz, ny = lax.axis_size("tx"), lax.axis_size("tz"), lax.axis_size("ty")
    boxes = loc_local.shape[0]
    ymean = jnp.mean(ens_obs, axis=1, dtype=jnp.float32)
    anomaly = (ens_obs.astype(jnp.float32) - ymean[:, None]).astype(jnp.bfloat16)
    inv_var = (1.0 / obs_var).astype(jnp.bfloat16)
    innov = (obs_values - ymean).astype(jnp.bfloat16)
    def edge_payload(index):
        info = jnp.concatenate([inv_var[index], innov[index]])
        info = jnp.pad(info, (0, members - info.shape[0]))
        return jnp.concatenate([anomaly[index], info[None]], axis=0)

    lower = passed_along(edge_payload(edge_up), "region", 1)
    upper = passed_along(edge_payload(edge_down), "region", -1)
    edge = edge_up.shape[0]
    lower_a, lower_v, lower_i = lower[:edge], lower[edge, :edge], lower[edge, edge:2 * edge]
    upper_a, upper_v, upper_i = upper[:edge], upper[edge, :edge], upper[edge, edge:2 * edge]
    edge_rows = lower_a.shape[0] + upper_a.shape[0]
    pool_rows = record_count + edge_rows
    block_rows = ((pool_rows + 1 + 15) // 16) * 16
    info_row = jnp.concatenate(
        [inv_var, lower_v, upper_v, innov, lower_i, upper_i,
         jnp.zeros((members - 2 * pool_rows,), jnp.bfloat16)])
    block = jnp.concatenate(
        [anomaly, lower_a, upper_a, info_row[None],
         jnp.zeros((block_rows - pool_rows - 1, members), jnp.bfloat16)], axis=0)
    half = lax.all_gather(block, "tz", axis=0)
    full = lax.all_gather(half, ("tx", "ty"), axis=0)
    info = full[:, :, pool_rows, :2 * pool_rows].astype(jnp.float32)
    inv_all = info[:, :, :pool_rows]
    innov_all = info[:, :, pool_rows:]
    local_w = loc_local.reshape(boxes, nx, nz, ny, record_count)
    edge_w = loc_edge.reshape(boxes, nx, nz, ny, edge_rows)
    weights = jnp.concatenate([local_w, edge_w], axis=4).transpose(0, 1, 3, 2, 4)
    weights = weights.reshape(boxes, nx * ny, nz, pool_rows)
    obs_scale = weights * inv_all[None]
    weighted = (obs_scale * innov_all[None]).astype(jnp.bfloat16)
    pad = ((0, 0), (0, 0), (0, 0), (0, block_rows - pool_rows))
    scale_rows = jnp.pad(obs_scale, pad).reshape(boxes, -1)
    scale_rows = jnp.pad(scale_rows, ((0, 8 - boxes), (0, 0)))
    weighted = jnp.pad(weighted, pad).reshape(boxes, -1)
    weighted = jnp.pad(weighted, ((0, 16 - boxes), (0, 0)))
    gram, innov_sum = gram_terms(full.reshape(-1, members), scale_rows, weighted, boxes)
    return analysis_of(gram, innov_sum, states, box_ids.reshape(-1, 1))


def solution(mesh):
    n_region, n_tile = mesh.devices.shape
    nz = 2
    nx = 4
    ny = n_tile // (nx * nz)
    fine = Mesh(mesh.devices.reshape(n_region, nx, nz, ny), ("region", "tx", "tz", "ty"))
    flat = ("region", "tx", "tz", "ty")
    return jax.shard_map(
        body,
        mesh=fine,
        in_specs=(
            P(flat, None),
            P(flat),
            P(flat),
            P(flat),
            P(flat),
            P(flat, None),
            P(flat, None),
            P(None, flat, None),
            P(flat),
        ),
        out_specs=P(None, flat, None),
        check_vma=False,
    )
```

```python
import functools

import jax
import jax.numpy as jnp
from jax import lax
from jax.experimental import pallas as pl
from jax.experimental.pallas import tpu as pltpu
from jax.sharding import Mesh
from jax.sharding import PartitionSpec as P

HI = lax.Precision.HIGHEST
ROWS_PER_STEP = 3328


def passed_along(block, axis, distance):
    devices = range(lax.axis_size(axis))
    route = [(i - distance, i) for i in devices if i - distance in devices]
    return lax.ppermute(block, axis, route)


def _gram_kernel(a_ref, s_ref, w_ref, g_ref, v_ref):
    @pl.when(pl.program_id(0) == 0)
    def _():
        g_ref[...] = jnp.zeros(g_ref.shape, jnp.float32)
        v_ref[...] = jnp.zeros(v_ref.shape, jnp.float32)

    a = a_ref[...]
    at = a.T.astype(jnp.float32)
    for b in range(g_ref.shape[0]):
        sct = (at * s_ref[b:b + 1, :]).astype(jnp.bfloat16)
        g_ref[b] += jnp.dot(sct, a, preferred_element_type=jnp.float32)
    v_ref[...] += jnp.dot(w_ref[...], a, preferred_element_type=jnp.float32)


def gram_terms(pool, scale_rows, weighted, gram_boxes):
    rows, members = pool.shape
    boxes = gram_boxes
    srows = scale_rows.shape[0]
    wrows = weighted.shape[0]
    step = ROWS_PER_STEP
    return pl.pallas_call(
        _gram_kernel,
        grid=(rows // step,),
        in_specs=[
            pl.BlockSpec((step, members), lambda i: (i, 0)),
            pl.BlockSpec((srows, step), lambda i: (0, i)),
            pl.BlockSpec((wrows, step), lambda i: (0, i)),
        ],
        out_specs=[
            pl.BlockSpec((boxes, members, members), lambda i: (0, 0, 0)),
            pl.BlockSpec((wrows, members), lambda i: (0, 0)),
        ],
        out_shape=[
            jax.ShapeDtypeStruct((boxes, members, members), jnp.float32),
            jax.ShapeDtypeStruct((wrows, members), jnp.float32),
        ],
    )(pool, scale_rows, weighted)


def _transform_kernel(g_ref, v_ref, s_ref, box_ref, o_ref, t_ref, m_ref, r_ref, *, nb):
    boxes, n, _ = g_ref.shape
    ridx = lax.broadcasted_iota(jnp.int32, (n, n), 0)
    cidx = lax.broadcasted_iota(jnp.int32, (n, n), 1)
    eye = (ridx == cidx).astype(jnp.float32)
    for b in range(boxes):
        m_ref[b] = g_ref[b] + (n - 1.0) * eye
    width = 4
    sub8 = lax.broadcasted_iota(jnp.int32, (8, nb), 0)
    lane8 = lax.broadcasted_iota(jnp.int32, (8, nb), 1)
    sub1 = lax.broadcasted_iota(jnp.int32, (8, 1), 0)
    bi = lax.broadcasted_iota(jnp.int32, (nb, nb), 0)
    bj = lax.broadcasted_iota(jnp.int32, (nb, nb), 1)
    beye = (bi == bj).astype(jnp.float32)

    def mul2(x, y):
        return [[x[i][0] * y[0][j] + x[i][1] * y[1][j] for j in range(2)] for i in range(2)]

    def inv2(x):
        r = 1.0 / (x[0][0] * x[1][1] - x[0][1] * x[1][0])
        return [[x[1][1] * r, -x[0][1] * r], [-x[1][0] * r, x[0][0] * r]]

    def pivot(step, blocks):
        k = width * step
        rmask = [bi == k + m for m in range(width)]
        lmask = [bj[0:1] == k + m for m in range(width)]
        out = []
        grp = (bi // 8) == (k // 8)
        kk = k % 8
        for d in blocks:
            g8 = jnp.sum(jnp.where(grp, d, 0.0).reshape(nb // 8, 8, nb), axis=0)
            rows = [jnp.sum(jnp.where(sub8 == kk + m, g8, 0.0), axis=0, keepdims=True) for m in range(width)]
            cols = [jnp.sum(jnp.where(bj == k + m, d, 0.0), axis=1, keepdims=True) for m in range(width)]
            pcol = [jnp.sum(jnp.where(lane8 == k + j, g8, 0.0), axis=1, keepdims=True) for j in range(width)]
            p = [[jnp.sum(jnp.where(sub1 == kk + i, pcol[j], 0.0), axis=0, keepdims=True)
                  for j in range(width)] for i in range(width)]
            a = [[p[0][0], p[0][1]], [p[1][0], p[1][1]]]
            b = [[p[0][2], p[0][3]], [p[1][2], p[1][3]]]
            c = [[p[2][0], p[2][1]], [p[3][0], p[3][1]]]
            e = [[p[2][2], p[2][3]], [p[3][2], p[3][3]]]
            ai = inv2(a)
            aib = mul2(ai, b)
            cai = mul2(c, ai)
            cab = mul2(c, aib)
            si = inv2([[e[i][j] - cab[i][j] for j in range(2)] for i in range(2)])
            q12 = [[-v for v in row] for row in mul2(aib, si)]
            q21 = [[-v for v in row] for row in mul2(si, cai)]
            q12c = mul2(q12, cai)
            q11 = [[ai[i][j] - q12c[i][j] for j in range(2)] for i in range(2)]
            q = [q11[0] + q12[0], q11[1] + q12[1], q21[0] + si[0], q21[1] + si[1]]
            new = d
            gs = []
            for i in range(width):
                rn = q[i][0] * rows[0]
                for j in range(1, width):
                    rn = rn + q[i][j] * rows[j]
                f, g = rn, rn
                for j in range(width):
                    f = jnp.where(lmask[j], q[i][j] + (1.0 if i == j else 0.0), f)
                    g = jnp.where(lmask[j], q[i][j], g)
                new = new - cols[i] * f
                gs.append(g)
            for i in range(width):
                new = jnp.where(rmask[i], gs[i], new)
            out.append(new)
        return tuple(out)

    for kb in range(n // nb):
        s = slice(kb * nb, (kb + 1) * nb)
        dinvs = lax.fori_loop(0, nb // width, pivot, tuple(m_ref[b, s, s] for b in range(boxes)))
        for b in range(boxes):
            dinv = dinvs[b]
            rn = jnp.dot(dinv, m_ref[b, s, :], precision=HI, preferred_element_type=jnp.float32)
            r_ref[b] = rn
            r_ref[b, :, s] = beye + dinv
            upd = jnp.dot(m_ref[b, :, s], r_ref[b], precision=HI, preferred_element_type=jnp.float32)
            m_ref[b] = m_ref[b] - upd
            m_ref[b, s, :] = rn
            m_ref[b, s, s] = dinv
    for b in range(boxes):
        inv = m_ref[b]
        wbar = jnp.sum(inv * v_ref[b:b + 1, :], axis=1, keepdims=True)
        t_ref[b] = (0.5 * eye + (0.5 * (n - 1.0)) * inv + wbar).astype(t_ref.dtype)
    box = box_ref[...]
    for f in range(s_ref.shape[0]):
        wide = s_ref[f].astype(jnp.float32)
        smean = jnp.sum(wide, axis=1, keepdims=True) / n
        anomaly = (wide - smean).astype(jnp.bfloat16)
        total = jnp.zeros(wide.shape, jnp.float32)
        for b in range(boxes):
            upd = jnp.dot(anomaly, t_ref[b], preferred_element_type=jnp.float32)
            total = total + jnp.where(box == b, upd, 0.0)
        o_ref[f] = (smean + total).astype(o_ref.dtype)


def analysis_of(gram, innov_rows, states, box_col, nb=64):
    boxes, n, _ = gram.shape
    return pl.pallas_call(
        functools.partial(_transform_kernel, nb=nb),
        out_shape=jax.ShapeDtypeStruct(states.shape, states.dtype),
        scratch_shapes=[pltpu.VMEM((boxes, n, n), jnp.bfloat16),
                        pltpu.VMEM((boxes, n, n), jnp.float32),
                        pltpu.VMEM((boxes, nb, n), jnp.float32)],
    )(gram, innov_rows, states, box_col)


def body(ens_obs, obs_values, obs_var, edge_up, edge_down, loc_local, loc_edge, states, box_ids):
    record_count, members = ens_obs.shape
    nx, nz, ny = lax.axis_size("tx"), lax.axis_size("tz"), lax.axis_size("ty")
    boxes = loc_local.shape[0]
    ymean = jnp.mean(ens_obs, axis=1, dtype=jnp.float32)
    anomaly = (ens_obs.astype(jnp.float32) - ymean[:, None]).astype(jnp.bfloat16)
    inv_var = (1.0 / obs_var).astype(jnp.bfloat16)
    innov = (obs_values - ymean).astype(jnp.bfloat16)
    def edge_payload(index):
        info = jnp.concatenate([inv_var[index], innov[index]])
        info = jnp.pad(info, (0, members - info.shape[0]))
        return jnp.concatenate([anomaly[index], info[None]], axis=0)

    lower = passed_along(edge_payload(edge_up), "region", 1)
    upper = passed_along(edge_payload(edge_down), "region", -1)
    edge = edge_up.shape[0]
    lower_a, lower_v, lower_i = lower[:edge], lower[edge, :edge], lower[edge, edge:2 * edge]
    upper_a, upper_v, upper_i = upper[:edge], upper[edge, :edge], upper[edge, edge:2 * edge]
    edge_rows = lower_a.shape[0] + upper_a.shape[0]
    pool_rows = record_count + edge_rows
    block_rows = ((pool_rows + 1 + 15) // 16) * 16
    info_row = jnp.concatenate(
        [inv_var, lower_v, upper_v, innov, lower_i, upper_i,
         jnp.zeros((members - 2 * pool_rows,), jnp.bfloat16)])
    block = jnp.concatenate(
        [anomaly, lower_a, upper_a, info_row[None],
         jnp.zeros((block_rows - pool_rows - 1, members), jnp.bfloat16)], axis=0)
    half = lax.all_gather(block, "tz", axis=0)
    full = lax.all_gather(half, ("tx", "ty"), axis=0)
    info = full[:, :, pool_rows, :2 * pool_rows].astype(jnp.float32)
    inv_all = info[:, :, :pool_rows]
    innov_all = info[:, :, pool_rows:]
    local_w = loc_local.reshape(boxes, nx, nz, ny, record_count)
    edge_w = loc_edge.reshape(boxes, nx, nz, ny, edge_rows)
    weights = jnp.concatenate([local_w, edge_w], axis=4).transpose(0, 1, 3, 2, 4)
    weights = weights.reshape(boxes, nx * ny, nz, pool_rows)
    obs_scale = weights * inv_all[None]
    weighted = (obs_scale * innov_all[None]).astype(jnp.bfloat16)
    pad = ((0, 0), (0, 0), (0, 0), (0, block_rows - pool_rows))
    scale_rows = jnp.pad(obs_scale, pad).reshape(boxes, -1)
    scale_rows = jnp.pad(scale_rows, ((0, 8 - boxes), (0, 0)))
    weighted = jnp.pad(weighted, pad).reshape(boxes, -1)
    weighted = jnp.pad(weighted, ((0, 16 - boxes), (0, 0)))
    gram, innov_sum = gram_terms(full.reshape(-1, members), scale_rows, weighted, boxes)
    return analysis_of(gram, innov_sum, states, box_ids.reshape(-1, 1))


def solution(mesh):
    n_region, n_tile = mesh.devices.shape
    nz = 2
    nx = 4
    ny = n_tile // (nx * nz)
    fine = Mesh(mesh.devices.reshape(n_region, nx, nz, ny), ("region", "tx", "tz", "ty"))
    flat = ("region", "tx", "tz", "ty")
    return jax.shard_map(
        body,
        mesh=fine,
        in_specs=(
            P(flat, None),
            P(flat),
            P(flat),
            P(flat),
            P(flat),
            P(flat, None),
            P(flat, None),
            P(None, flat, None),
            P(flat),
        ),
        out_specs=P(None, flat, None),
        check_vma=False,
    )
```

```python
import functools

import jax
import jax.numpy as jnp
from jax import lax
from jax.experimental import pallas as pl
from jax.experimental.pallas import tpu as pltpu
from jax.sharding import Mesh
from jax.sharding import PartitionSpec as P

HI = lax.Precision.HIGHEST
ROWS_PER_STEP = 3328


def passed_along(block, axis, distance):
    devices = range(lax.axis_size(axis))
    route = [(i - distance, i) for i in devices if i - distance in devices]
    return lax.ppermute(block, axis, route)


def _gram_kernel(a_ref, s_ref, w_ref, g_ref, v_ref):
    @pl.when(pl.program_id(0) == 0)
    def _():
        g_ref[...] = jnp.zeros(g_ref.shape, jnp.float32)
        v_ref[...] = jnp.zeros(v_ref.shape, jnp.float32)

    a = a_ref[...]
    at = a.T.astype(jnp.float32)
    for b in range(g_ref.shape[0]):
        sct = (at * s_ref[b:b + 1, :]).astype(jnp.bfloat16)
        g_ref[b] += jnp.dot(sct, a, preferred_element_type=jnp.float32)
    v_ref[...] += jnp.dot(w_ref[...], a, preferred_element_type=jnp.float32)


def gram_terms(pool, scale_rows, weighted, gram_boxes):
    rows, members = pool.shape
    boxes = gram_boxes
    srows = scale_rows.shape[0]
    wrows = weighted.shape[0]
    step = ROWS_PER_STEP
    return pl.pallas_call(
        _gram_kernel,
        grid=(rows // step,),
        in_specs=[
            pl.BlockSpec((step, members), lambda i: (i, 0)),
            pl.BlockSpec((srows, step), lambda i: (0, i)),
            pl.BlockSpec((wrows, step), lambda i: (0, i)),
        ],
        out_specs=[
            pl.BlockSpec((boxes, members, members), lambda i: (0, 0, 0)),
            pl.BlockSpec((wrows, members), lambda i: (0, 0)),
        ],
        out_shape=[
            jax.ShapeDtypeStruct((boxes, members, members), jnp.float32),
            jax.ShapeDtypeStruct((wrows, members), jnp.float32),
        ],
    )(pool, scale_rows, weighted)


def _transform_kernel(g_ref, v_ref, s_ref, box_ref, o_ref, t_ref, m_ref, r_ref, *, nb):
    boxes, n, _ = g_ref.shape
    ridx = lax.broadcasted_iota(jnp.int32, (n, n), 0)
    cidx = lax.broadcasted_iota(jnp.int32, (n, n), 1)
    eye = (ridx == cidx).astype(jnp.float32)
    for b in range(boxes):
        m_ref[b] = g_ref[b] + (n - 1.0) * eye
    width = 4
    sub8 = lax.broadcasted_iota(jnp.int32, (8, nb), 0)
    lane8 = lax.broadcasted_iota(jnp.int32, (8, nb), 1)
    sub1 = lax.broadcasted_iota(jnp.int32, (8, 1), 0)
    bi = lax.broadcasted_iota(jnp.int32, (nb, nb), 0)
    bj = lax.broadcasted_iota(jnp.int32, (nb, nb), 1)
    beye = (bi == bj).astype(jnp.float32)

    def mul2(x, y):
        return [[x[i][0] * y[0][j] + x[i][1] * y[1][j] for j in range(2)] for i in range(2)]

    def inv2(x):
        r = 1.0 / (x[0][0] * x[1][1] - x[0][1] * x[1][0])
        return [[x[1][1] * r, -x[0][1] * r], [-x[1][0] * r, x[0][0] * r]]

    def pivot(step, blocks):
        k = width * step
        rmask = [bi == k + m for m in range(width)]
        lmask = [bj[0:1] == k + m for m in range(width)]
        out = []
        grp = (bi // 8) == (k // 8)
        kk = k % 8
        for d in blocks:
            g8 = jnp.sum(jnp.where(grp, d, 0.0).reshape(nb // 8, 8, nb), axis=0)
            rows = [jnp.sum(jnp.where(sub8 == kk + m, g8, 0.0), axis=0, keepdims=True) for m in range(width)]
            cols = [jnp.sum(jnp.where(bj == k + m, d, 0.0), axis=1, keepdims=True) for m in range(width)]
            pcol = [jnp.sum(jnp.where(lane8 == k + j, g8, 0.0), axis=1, keepdims=True) for j in range(width)]
            p = [[jnp.sum(jnp.where(sub1 == kk + i, pcol[j], 0.0), axis=0, keepdims=True)
                  for j in range(width)] for i in range(width)]
            a = [[p[0][0], p[0][1]], [p[1][0], p[1][1]]]
            b = [[p[0][2], p[0][3]], [p[1][2], p[1][3]]]
            c = [[p[2][0], p[2][1]], [p[3][0], p[3][1]]]
            e = [[p[2][2], p[2][3]], [p[3][2], p[3][3]]]
            ai = inv2(a)
            aib = mul2(ai, b)
            cai = mul2(c, ai)
            cab = mul2(c, aib)
            si = inv2([[e[i][j] - cab[i][j] for j in range(2)] for i in range(2)])
            q12 = [[-v for v in row] for row in mul2(aib, si)]
            q21 = [[-v for v in row] for row in mul2(si, cai)]
            q12c = mul2(q12, cai)
            q11 = [[ai[i][j] - q12c[i][j] for j in range(2)] for i in range(2)]
            q = [q11[0] + q12[0], q11[1] + q12[1], q21[0] + si[0], q21[1] + si[1]]
            new = d
            gs = []
            for i in range(width):
                rn = q[i][0] * rows[0]
                for j in range(1, width):
                    rn = rn + q[i][j] * rows[j]
                f, g = rn, rn
                for j in range(width):
                    f = jnp.where(lmask[j], q[i][j] + (1.0 if i == j else 0.0), f)
                    g = jnp.where(lmask[j], q[i][j], g)
                new = new - cols[i] * f
                gs.append(g)
            for i in range(width):
                new = jnp.where(rmask[i], gs[i], new)
            out.append(new)
        return tuple(out)

    for kb in range(n // nb):
        s = slice(kb * nb, (kb + 1) * nb)
        dinvs = lax.fori_loop(0, nb // width, pivot, tuple(m_ref[b, s, s] for b in range(boxes)))
        for b in range(boxes):
            dinv = dinvs[b]
            rn = jnp.dot(dinv, m_ref[b, s, :], precision=HI, preferred_element_type=jnp.float32)
            r_ref[b] = rn
            r_ref[b, :, s] = beye + dinv
            upd = jnp.dot(m_ref[b, :, s], r_ref[b], precision=HI, preferred_element_type=jnp.float32)
            m_ref[b] = m_ref[b] - upd
            m_ref[b, s, :] = rn
            m_ref[b, s, s] = dinv
    for b in range(boxes):
        inv = m_ref[b]
        wbar = jnp.sum(inv * v_ref[b:b + 1, :], axis=1, keepdims=True)
        t_ref[b] = (0.5 * eye + (0.5 * (n - 1.0)) * inv + wbar).astype(t_ref.dtype)
    box = box_ref[...]
    for f in range(s_ref.shape[0]):
        wide = s_ref[f].astype(jnp.float32)
        smean = jnp.sum(wide, axis=1, keepdims=True) / n
        anomaly = (wide - smean).astype(jnp.bfloat16)
        total = jnp.zeros(wide.shape, jnp.float32)
        for b in range(boxes):
            upd = jnp.dot(anomaly, t_ref[b], preferred_element_type=jnp.float32)
            total = total + jnp.where(box == b, upd, 0.0)
        o_ref[f] = (smean + total).astype(o_ref.dtype)


def analysis_of(gram, innov_rows, states, box_col, nb=64):
    boxes, n, _ = gram.shape
    return pl.pallas_call(
        functools.partial(_transform_kernel, nb=nb),
        out_shape=jax.ShapeDtypeStruct(states.shape, states.dtype),
        scratch_shapes=[pltpu.VMEM((boxes, n, n), jnp.bfloat16),
                        pltpu.VMEM((boxes, n, n), jnp.float32),
                        pltpu.VMEM((boxes, nb, n), jnp.float32)],
    )(gram, innov_rows, states, box_col)


def body(ens_obs, obs_values, obs_var, edge_up, edge_down, loc_local, loc_edge, states, box_ids):
    record_count, members = ens_obs.shape
    nx, nz, ny = lax.axis_size("tx"), lax.axis_size("tz"), lax.axis_size("ty")
    boxes = loc_local.shape[0]
    ymean = jnp.mean(ens_obs, axis=1, dtype=jnp.float32)
    anomaly = (ens_obs.astype(jnp.float32) - ymean[:, None]).astype(jnp.bfloat16)
    inv_var = (1.0 / obs_var).astype(jnp.bfloat16)
    innov = (obs_values - ymean).astype(jnp.bfloat16)
    def edge_payload(index):
        info = jnp.concatenate([inv_var[index], innov[index]])
        info = jnp.pad(info, (0, members - info.shape[0]))
        return jnp.concatenate([anomaly[index], info[None]], axis=0)

    edge = edge_up.shape[0]
    n_region = lax.axis_size("region")
    up_payload, down_payload = edge_payload(edge_up), edge_payload(edge_down)
    cross_up = [(r * nz + t, (r + 1) * nz + (1 - t)) for r in range(n_region - 1) for t in range(nz)]
    cross_down = [((r + 1) * nz + t, r * nz + (1 - t)) for r in range(n_region - 1) for t in range(nz)]
    same = (passed_along(up_payload, "region", 1), passed_along(down_payload, "region", -1))
    cross = (lax.ppermute(up_payload, ("region", "tz"), cross_up),
             lax.ppermute(down_payload, ("region", "tz"), cross_down))
    own_info = jnp.pad(jnp.concatenate([inv_var, innov]), (0, members - 2 * record_count))
    own = jnp.concatenate([anomaly, own_info[None]], axis=0)
    own_half = lax.all_gather(own, "tz", axis=0)
    edge_rows = 2 * edge
    pool_rows = record_count + edge_rows
    block_rows = ((pool_rows + 1 + 15) // 16) * 16
    tz_at = lax.axis_index("tz")
    blocks = []
    for k in range(nz):
        lower, upper = [jnp.where(tz_at == k, s, c) for s, c in zip(same, cross)]
        info = own_half[k, record_count]
        info_row = jnp.concatenate(
            [info[:record_count], lower[edge, :edge], upper[edge, :edge],
             info[record_count:2 * record_count], lower[edge, edge:2 * edge], upper[edge, edge:2 * edge],
             jnp.zeros((members - 2 * pool_rows,), jnp.bfloat16)])
        blocks.append(jnp.concatenate(
            [own_half[k, :record_count], lower[:edge], upper[:edge], info_row[None],
             jnp.zeros((block_rows - pool_rows - 1, members), jnp.bfloat16)], axis=0))
    half = jnp.stack(blocks)
    full = lax.all_gather(half, ("tx", "ty"), axis=0)
    info = full[:, :, pool_rows, :2 * pool_rows].astype(jnp.float32)
    inv_all = info[:, :, :pool_rows]
    innov_all = info[:, :, pool_rows:]
    local_w = loc_local.reshape(boxes, nx, nz, ny, record_count)
    edge_w = loc_edge.reshape(boxes, nx, nz, ny, edge_rows)
    weights = jnp.concatenate([local_w, edge_w], axis=4).transpose(0, 1, 3, 2, 4)
    weights = weights.reshape(boxes, nx * ny, nz, pool_rows)
    obs_scale = weights * inv_all[None]
    weighted = (obs_scale * innov_all[None]).astype(jnp.bfloat16)
    pad = ((0, 0), (0, 0), (0, 0), (0, block_rows - pool_rows))
    scale_rows = jnp.pad(obs_scale, pad).reshape(boxes, -1)
    scale_rows = jnp.pad(scale_rows, ((0, 8 - boxes), (0, 0)))
    weighted = jnp.pad(weighted, pad).reshape(boxes, -1)
    weighted = jnp.pad(weighted, ((0, 16 - boxes), (0, 0)))
    gram, innov_sum = gram_terms(full.reshape(-1, members), scale_rows, weighted, boxes)
    return analysis_of(gram, innov_sum, states, box_ids.reshape(-1, 1))


def solution(mesh):
    n_region, n_tile = mesh.devices.shape
    nz = 2
    nx = 4
    ny = n_tile // (nx * nz)
    fine = Mesh(mesh.devices.reshape(n_region, nx, nz, ny), ("region", "tx", "tz", "ty"))
    flat = ("region", "tx", "tz", "ty")
    return jax.shard_map(
        body,
        mesh=fine,
        in_specs=(
            P(flat, None),
            P(flat),
            P(flat),
            P(flat),
            P(flat),
            P(flat, None),
            P(flat, None),
            P(None, flat, None),
            P(flat),
        ),
        out_specs=P(None, flat, None),
        check_vma=False,
    )
```
